512 devices in a mesh: layer: 64 (over y, z_lo, x), batch: 8 (over z_hi, core).
Axes of the slice: x: 4, y: 4, z: 16 (z_hi: 4, z_lo: 4; z = z_hi * 4 + z_lo), core: 2. Of those that a mesh axis runs over, the one named last changes fastest.
Arguments:
- initial_state: float32 [8, 128, 512], P('batch'), may hold values from -6 to 6
- cotangent: float32 [8, 128, 512], P('batch'), may hold values from -6 to 6
- conv_weight: bfloat16 [128, 128, 1152], P('layer'), may hold values from -0.1875 to 0.1875
- conv_bias: float32 [128, 128], P('layer'), may hold values from -3 to 3
- block_gain: float32 [64, 128], P('layer'), may hold values from 0 to 1
- adjoint_gain: float32 [64, 128], P('layer'), may hold values from 0 to 1
Outputs:
- block_ends: float32 [64, 8, 128, 512], P('layer', 'batch')
- adjoint_start: float32 [64, 8, 128, 512], P('layer', 'batch')
- weight_grad: float32 [128, 128, 1152], P('layer')
- bias_grad: float32 [128, 128], P('layer')
The draws below stay inside these ranges and needn't reach their ends.
All inputs are finite; a program needn't handle non-finite values.
Results may differ from the reference program's by a relative error of at most 0.0085.
Values sent between devices are 32-bit elements; how exact they have to be, the bound alone decides.
No kernel may reach another device: no remote copies, remote signals or barrier semaphores. Data moves between devices by JAX's collectives and lax.ppermute only.
A program may use at most 64 MiB of HBM per device.

```python
import jax
import jax.numpy as jnp
from jax import lax

FEATURE_DEPTH = 128
HEIGHT = 16
WIDTH = 32
L_DEV = 2
ITERS = 2
PIX = 512
COARSE_INTERVALS = 64
LAYERS = 128
BATCH = 8


def gain_table(key):
    indicator_random_seed, gradual_random_seed, quick_random_seed, changing_random_seed, location_random_seed, spike_random_seed = jax.random.split(key, 6)
    gradual_indicator = jax.random.randint(indicator_random_seed, (FEATURE_DEPTH,), 0, 2) == 1
    slow_rate = jnp.exp(jax.random.uniform(gradual_random_seed, (FEATURE_DEPTH,), jnp.float32, jnp.log(0.1), jnp.log(0.5))) / COARSE_INTERVALS
    fast_rate = jnp.exp(jax.random.uniform(quick_random_seed, (FEATURE_DEPTH,), jnp.float32, jnp.log(0.7), jnp.log(1.6)))
    rate_row = jnp.where(gradual_indicator, slow_rate, fast_rate)
    varying = jnp.exp(jax.random.uniform(changing_random_seed, (COARSE_INTERVALS, FEATURE_DEPTH), jnp.float32, jnp.log(0.6), jnp.log(1.6)))
    spots = jax.random.randint(location_random_seed, (2,), 0, COARSE_INTERVALS)
    perturbed_locations = jnp.any(jnp.arange(COARSE_INTERVALS)[:, None] == spots[None, :], axis=1)
    spike_number = jax.random.uniform(spike_random_seed, (COARSE_INTERVALS, FEATURE_DEPTH), jnp.float32, 0.5, 0.8)
    interval_stride = jnp.where(perturbed_locations[:, None] & gradual_indicator[None, :], spike_number, jnp.ones_like(spike_number))
    return (jnp.exp(-rate_row[None, :] * varying) * interval_stride).astype(jnp.float32)


def draw_block_gain(key, part):
    return gain_table(jax.random.fold_in(key, 11))


def draw_adjoint_gain(key, part):
    return gain_table(jax.random.fold_in(key, 23))


def shard_levels(rng, shape, cuts, least, top_value):
    factor_of = 1.0
    for axis_at, blocks in cuts:
        steps = jax.random.uniform(jax.random.fold_in(jax.random.fold_in(rng, 6), axis_at), (blocks,), jnp.float32, least / len(cuts), top_value / len(cuts))
        factor_of = factor_of * jnp.repeat(jnp.exp(steps), shape[axis_at] // blocks).reshape((-1,) + (1,) * (len(shape) - 1 - axis_at))
    return factor_of


def centred(rng, extent, deviation, most, shards=(), held_as=jnp.bfloat16):
    drawn = jax.random.normal(rng, extent, jnp.float32) * deviation
    if len(shards) > 0:
        drawn = shard_levels(rng, extent, shards, -0.22, 0.18) * drawn
    return jnp.clip(drawn, min=-most, max=most).astype(held_as)


def setup_inputs(seed: int = 0) -> dict:
    keys = jax.random.split(jax.random.key(seed), 7)
    initial_state = centred(keys[0], (BATCH, FEATURE_DEPTH, PIX), 1.0, 6.0, ((0, 8),), jnp.float32)
    cotangent = centred(keys[1], (BATCH, FEATURE_DEPTH, PIX), 1.0, 6.0, ((0, 8),), jnp.float32)
    conv_weight = centred(keys[2], (LAYERS, FEATURE_DEPTH, 9 * FEATURE_DEPTH), (9 * FEATURE_DEPTH) ** -0.5, 0.1875, ((0, 64),))
    conv_bias = centred(keys[3], (LAYERS, FEATURE_DEPTH), 0.5, 3.0, ((0, 64),), jnp.float32)
    block_gain = draw_block_gain(jax.random.fold_in(keys[6], 71), 0)
    adjoint_gain = draw_adjoint_gain(jax.random.fold_in(keys[6], 71), 0)
    return dict(initial_state=initial_state, cotangent=cotangent, conv_weight=conv_weight, conv_bias=conv_bias, block_gain=block_gain, adjoint_gain=adjoint_gain)


step_size = 0.25


def columns(current):
    rounded = current.astype(jnp.bfloat16)
    pixels = HEIGHT * WIDTH
    margin = WIDTH + 1
    padded = jnp.pad(rounded, ((0, 0), (0, 0), (margin, margin)))
    across = jnp.arange(pixels) % WIDTH
    pieces = []
    for offset_y in (-1, 0, 1):
        for offset_x in (-1, 0, 1):
            shift_by = offset_y * WIDTH + offset_x
            inside = (across + offset_x >= 0) & (across + offset_x < WIDTH)
            window = padded[:, :, margin + shift_by:margin + shift_by + pixels]
            pieces.append(jnp.where(inside, window, jnp.zeros_like(window)))
    return jnp.concatenate(pieces, axis=1)


def uncolumns(spread):
    channels = spread.shape[1] // 9
    pixels = HEIGHT * WIDTH
    margin = WIDTH + 1
    across = jnp.arange(pixels) % WIDTH
    summed = jnp.zeros((spread.shape[0], channels, pixels), jnp.float32)
    tap_index = 0
    for offset_y in (-1, 0, 1):
        for offset_x in (-1, 0, 1):
            shift_by = offset_y * WIDTH + offset_x
            inside = (across + offset_x >= 0) & (across + offset_x < WIDTH)
            window = spread[:, tap_index * channels:(tap_index + 1) * channels]
            masked = jnp.where(inside, window, jnp.zeros_like(window))
            placed = jnp.pad(masked, ((0, 0), (0, 0), (margin + shift_by, margin - shift_by)))
            summed = summed + placed[:, :, margin:margin + pixels]
            tap_index = tap_index + 1
    return summed


def forward_layer(current, weight, bias_row):
    stacked = columns(current)
    pre_act = jnp.einsum("ok,bkp->bop", weight.astype(jnp.float32), stacked.astype(jnp.float32),
                         precision=lax.Precision.HIGHEST) + bias_row[None, :, None]
    activity = jnp.tanh(pre_act)
    return current + step_size * activity, activity


def backward_layer(adjoint, activity, weight):
    scaled = step_size * (1.0 - activity * activity) * adjoint
    rounded = scaled.astype(jnp.bfloat16)
    spread = jnp.einsum("ok,bop->bkp", weight.astype(jnp.float32), rounded.astype(jnp.float32),
                        precision=lax.Precision.HIGHEST)
    return adjoint + uncolumns(spread), rounded, scaled


def reference(initial_state, cotangent, conv_weight, conv_bias, block_gain, adjoint_gain):
    weights = conv_weight.reshape(COARSE_INTERVALS, L_DEV, FEATURE_DEPTH, 9 * FEATURE_DEPTH)
    biases = conv_bias.reshape(COARSE_INTERVALS, L_DEV, FEATURE_DEPTH)
    zero_state = jnp.zeros_like(initial_state)

    def relax_one(packed):
        current, weight_block, bias_block = packed
        for layer_index in range(L_DEV):
            current, activity = forward_layer(current, weight_block[layer_index], bias_block[layer_index])
        return current

    def relax_keep(packed):
        current, weight_block, bias_block = packed
        input_list = []
        activity_list = []
        for layer_index in range(L_DEV):
            input_list.append(current)
            current, activity = forward_layer(current, weight_block[layer_index], bias_block[layer_index])
            activity_list.append(activity)
        return current, jnp.stack(input_list), jnp.stack(activity_list)

    def chain_step(error_now, packed):
        gain_row, residual = packed
        error_now = gain_row[None, :, None] * error_now + residual
        return error_now, error_now

    c_points = jnp.broadcast_to(initial_state[None], (COARSE_INTERVALS,) + initial_state.shape)
    for sweep_index in range(ITERS):
        endings = lax.map(relax_one, (c_points, weights, biases))
        residuals = endings[:-1] - c_points[1:]
        unused, errors = lax.scan(chain_step, zero_state, (block_gain[:-1], residuals))
        c_points = c_points + jnp.concatenate([zero_state[None], errors], axis=0)
    endings, inputs_all, activities = lax.map(relax_keep, (c_points, weights, biases))

    def adjoint_one(packed):
        adjoint, activity_block, weight_block = packed
        for layer_index in range(L_DEV - 1, -1, -1):
            adjoint = backward_layer(adjoint, activity_block[layer_index], weight_block[layer_index])[0]
        return adjoint

    def adjoint_keep(packed):
        adjoint, activity_block, input_block, weight_block = packed
        weight_parts = []
        bias_parts = []
        for layer_index in range(L_DEV - 1, -1, -1):
            adjoint, rounded, scaled = backward_layer(adjoint, activity_block[layer_index], weight_block[layer_index])
            stacked = columns(input_block[layer_index])
            weight_parts.insert(0, jnp.einsum("bop,bkp->ok", rounded.astype(jnp.float32), stacked.astype(jnp.float32),
                                              precision=lax.Precision.HIGHEST))
            bias_parts.insert(0, jnp.sum(scaled, axis=(0, 2)))
        return adjoint, jnp.stack(weight_parts), jnp.stack(bias_parts)

    targets = jnp.broadcast_to(cotangent[None], (COARSE_INTERVALS,) + cotangent.shape)
    for sweep_index in range(ITERS):
        starts = lax.map(adjoint_one, (targets, activities, weights))
        residuals = starts[1:] - targets[:-1]
        unused, errors = lax.scan(chain_step, zero_state, (adjoint_gain[1:], residuals), reverse=True)
        targets = targets + jnp.concatenate([errors, zero_state[None]], axis=0)
    starts, weight_grad, bias_grad = lax.map(adjoint_keep, (targets, activities, inputs_all, weights))
    return endings, starts, weight_grad.reshape(LAYERS, FEATURE_DEPTH, 9 * FEATURE_DEPTH), bias_grad.reshape(LAYERS, FEATURE_DEPTH)
```

```python
import jax
import jax.numpy as jnp
from jax import lax
from jax.sharding import PartitionSpec as P

HEIGHT = 16
WIDTH = 32
ITERS = 2


step_size = 0.25


def columns(current):
    rounded = current.astype(jnp.bfloat16)
    pixels = HEIGHT * WIDTH
    margin = WIDTH + 1
    padded = jnp.pad(rounded, ((0, 0), (0, 0), (margin, margin)))
    across = jnp.arange(pixels) % WIDTH
    pieces = []
    for offset_y in (-1, 0, 1):
        for offset_x in (-1, 0, 1):
            shift_by = offset_y * WIDTH + offset_x
            inside = (across + offset_x >= 0) & (across + offset_x < WIDTH)
            window = padded[:, :, margin + shift_by : margin + shift_by + pixels]
            pieces.append(jnp.where(inside, window, jnp.zeros_like(window)))
    return jnp.concatenate(pieces, axis=1)


def flip_weight(weight):
    channels = weight.shape[0]
    taps = weight.reshape(channels, 9, channels)[:, ::-1, :]
    return jnp.transpose(taps, (2, 1, 0)).reshape(channels, 9 * channels)


def forward_layer(current, weight, bias_row):
    stacked = columns(current)
    pre_act = (
        jnp.einsum("ok,bkp->bop", weight, stacked, preferred_element_type=jnp.float32)
        + bias_row[None, :, None]
    )
    activity = jnp.tanh(pre_act)
    return (current + step_size * activity, activity, stacked)


def backward_layer(adjoint, activity, flipped):
    scaled = step_size * (1.0 - activity * activity) * adjoint
    rounded = scaled.astype(jnp.bfloat16)
    gathered = columns(rounded)
    back = jnp.einsum("ck,bkp->bcp", flipped, gathered, preferred_element_type=jnp.float32)
    return (adjoint + back, rounded, scaled)


def relax_block(start, weights, biases):
    current = start
    stored = []
    for layer_index in range(weights.shape[0]):
        current, activity, stacked = forward_layer(
            current, weights[layer_index], biases[layer_index]
        )
        stored.append((stacked, activity))
    return (current, stored)


def adjoint_block(finish, stored, flipped_list):
    adjoint = finish
    for layer_index in range(len(stored) - 1, -1, -1):
        adjoint = backward_layer(adjoint, stored[layer_index][1], flipped_list[layer_index])[0]
    return adjoint


def window_products(table, place, distances):
    rows = jnp.arange(table.shape[0])
    out = []
    for d in distances:
        inside = (rows >= place - d + 1) & (rows <= place - 1)
        out.append(jnp.prod(jnp.where(inside[:, None], table, 1.0), axis=0))
    return out


def exclusive_scan(gain, local, table, place, axis, reverse):
    count = lax.axis_size(axis)
    distances = []
    d = 1
    while d < count:
        distances.append(d)
        d *= 2
    factors = window_products(table, place, distances)
    total = jnp.zeros_like(local)
    for d, factor in zip(distances, factors):
        sending = gain[None, :, None] * total + local
        if reverse:
            pairs = [(k, k - d) for k in range(d, count)]
        else:
            pairs = [(k, k + d) for k in range(count - d)]
        received = lax.ppermute(sending, axis, pairs)
        total = total + factor[None, :, None] * received
    return total


def per_device(initial_state, cotangent, conv_weight, conv_bias, block_gain, adjoint_gain):
    position = lax.axis_index("layer")
    blocks = lax.axis_size("layer")
    gain_row = block_gain[0]
    back_row = adjoint_gain[0]
    gain_table = lax.all_gather(gain_row, "layer")
    back_table = lax.all_gather(back_row, "layer")[::-1]
    flipped_list = [
        flip_weight(conv_weight[layer_index]) for layer_index in range(conv_weight.shape[0])
    ]
    c_points = initial_state
    following = initial_state
    for sweep_index in range(ITERS):
        ending = relax_block(c_points, conv_weight, conv_bias)[0]
        residual = ending - following
        error = exclusive_scan(gain_row, residual, gain_table, position, "layer", False)
        c_points = c_points + error
        following = following + gain_row[None, :, None] * error + residual
    ending, stored = relax_block(c_points, conv_weight, conv_bias)
    target = cotangent
    previous = cotangent
    for sweep_index in range(ITERS):
        start_adj = adjoint_block(target, stored, flipped_list)
        residual = start_adj - previous
        error = exclusive_scan(
            back_row, residual, back_table, blocks - 1 - position, "layer", True
        )
        target = target + error
        previous = previous + back_row[None, :, None] * error + residual
    adjoint = target
    weight_parts = []
    bias_parts = []
    for layer_index in range(len(stored) - 1, -1, -1):
        adjoint, rounded, scaled = backward_layer(
            adjoint, stored[layer_index][1], flipped_list[layer_index]
        )
        weight_part = jnp.einsum(
            "bop,bkp->ok", rounded, stored[layer_index][0], preferred_element_type=jnp.float32
        )
        bias_part = jnp.sum(scaled, axis=(0, 2))
        weight_parts.insert(0, weight_part)
        bias_parts.insert(0, bias_part)
    weight_grad = jnp.stack(weight_parts)
    bias_grad = jnp.stack(bias_parts)
    weight_grad, bias_grad = lax.psum((weight_grad, bias_grad), "batch")
    return (ending[None], adjoint[None], weight_grad, bias_grad)


def solution(mesh):
    return jax.shard_map(
        per_device,
        mesh=mesh,
        in_specs=(
            P("batch", None, None),
            P("batch", None, None),
            P("layer", None, None),
            P("layer", None),
            P("layer", None),
            P("layer", None),
        ),
        out_specs=(
            P("layer", "batch", None, None),
            P("layer", "batch", None, None),
            P("layer", None, None),
            P("layer", None),
        ),
        check_vma=False,
    )
```

```python
import jax
import jax.numpy as jnp
from jax import lax
from jax.sharding import PartitionSpec as P

HEIGHT = 16
WIDTH = 32
ITERS = 2


step_size = 0.25


def columns(current):
    rounded = current.astype(jnp.bfloat16)
    pixels = HEIGHT * WIDTH
    margin = WIDTH + 1
    padded = jnp.pad(rounded, ((0, 0), (0, 0), (margin, margin)))
    across = jnp.arange(pixels) % WIDTH
    pieces = []
    for offset_y in (-1, 0, 1):
        for offset_x in (-1, 0, 1):
            shift_by = offset_y * WIDTH + offset_x
            inside = (across + offset_x >= 0) & (across + offset_x < WIDTH)
            window = padded[:, :, margin + shift_by : margin + shift_by + pixels]
            pieces.append(jnp.where(inside, window, jnp.zeros_like(window)))
    return jnp.concatenate(pieces, axis=1)


def flip_weight(weight):
    channels = weight.shape[0]
    taps = weight.reshape(channels, 9, channels)[:, ::-1, :]
    return jnp.transpose(taps, (2, 1, 0)).reshape(channels, 9 * channels)


def forward_layer(current, weight, bias_row):
    stacked = columns(current)
    pre_act = (
        jnp.einsum("ok,bkp->bop", weight, stacked, preferred_element_type=jnp.float32)
        + bias_row[None, :, None]
    )
    activity = jnp.tanh(pre_act)
    return (current + step_size * activity, activity, stacked)


def backward_layer(adjoint, activity, flipped):
    scaled = step_size * (1.0 - activity * activity) * adjoint
    rounded = scaled.astype(jnp.bfloat16)
    gathered = columns(rounded)
    back = jnp.einsum("ck,bkp->bcp", flipped, gathered, preferred_element_type=jnp.float32)
    return (adjoint + back, rounded, scaled)


def relax_block(start, weights, biases):
    current = start
    stored = []
    for layer_index in range(weights.shape[0]):
        current, activity, stacked = forward_layer(
            current, weights[layer_index], biases[layer_index]
        )
        stored.append((stacked, activity))
    return (current, stored)


def adjoint_block(finish, stored, flipped_list):
    adjoint = finish
    for layer_index in range(len(stored) - 1, -1, -1):
        adjoint = backward_layer(adjoint, stored[layer_index][1], flipped_list[layer_index])[0]
    return adjoint


def scan_distances(count):
    distances = []
    d = 1
    while d < count:
        distances.append(d)
        d *= 2
    return distances


def scan_pairs(count, d, reverse):
    if reverse:
        return [(k, k - d) for k in range(d, count)]
    return [(k, k + d) for k in range(count - d)]


def exclusive_scan_first(gain, local, axis, reverse):
    count = lax.axis_size(axis)
    channels, pixels = local.shape[1], local.shape[2]
    total = jnp.zeros_like(local)
    product = jnp.ones_like(gain)
    factors = []
    for d in scan_distances(count):
        sending = gain[None, :, None] * total + local
        gain_row = jnp.pad(gain * product, (0, pixels - channels))
        packed = jnp.concatenate([sending, gain_row[None, None, :]], axis=1)
        received = lax.ppermute(packed, axis, scan_pairs(count, d, reverse))
        factors.append(product)
        total = total + product[None, :, None] * received[:, :channels, :]
        product = product * received[0, channels, :channels]
    return total, factors


def exclusive_scan_again(gain, local, factors, axis, reverse):
    count = lax.axis_size(axis)
    total = jnp.zeros_like(local)
    for d, factor in zip(scan_distances(count), factors):
        sending = gain[None, :, None] * total + local
        received = lax.ppermute(sending, axis, scan_pairs(count, d, reverse))
        total = total + factor[None, :, None] * received
    return total


def per_device(initial_state, cotangent, conv_weight, conv_bias, block_gain, adjoint_gain):
    gain_row = block_gain[0]
    back_row = adjoint_gain[0]
    flipped_list = [
        flip_weight(conv_weight[layer_index]) for layer_index in range(conv_weight.shape[0])
    ]
    c_points = initial_state
    following = initial_state
    for sweep_index in range(ITERS):
        ending = relax_block(c_points, conv_weight, conv_bias)[0]
        residual = ending - following
        if sweep_index == 0:
            error, factors = exclusive_scan_first(gain_row, residual, "layer", False)
        else:
            error = exclusive_scan_again(gain_row, residual, factors, "layer", False)
        c_points = c_points + error
        following = following + gain_row[None, :, None] * error + residual
    ending, stored = relax_block(c_points, conv_weight, conv_bias)
    target = cotangent
    previous = cotangent
    for sweep_index in range(ITERS):
        start_adj = adjoint_block(target, stored, flipped_list)
        residual = start_adj - previous
        if sweep_index == 0:
            error, factors = exclusive_scan_first(back_row, residual, "layer", True)
        else:
            error = exclusive_scan_again(back_row, residual, factors, "layer", True)
        target = target + error
        previous = previous + back_row[None, :, None] * error + residual
    adjoint = target
    weight_parts = []
    bias_parts = []
    for layer_index in range(len(stored) - 1, -1, -1):
        adjoint, rounded, scaled = backward_layer(
            adjoint, stored[layer_index][1], flipped_list[layer_index]
        )
        weight_part = jnp.einsum(
            "bop,bkp->ok", rounded, stored[layer_index][0], preferred_element_type=jnp.float32
        )
        bias_part = jnp.sum(scaled, axis=(0, 2))
        weight_parts.insert(0, weight_part)
        bias_parts.insert(0, bias_part)
    width = weight_parts[0].shape[1]
    channels = weight_parts[0].shape[0]
    packed = jnp.stack(
        [
            jnp.concatenate([w, jnp.pad(b, (0, width - channels))[None, :]], axis=0)
            for w, b in zip(weight_parts, bias_parts)
        ]
    )
    packed = lax.psum(packed, "batch")
    weight_grad = packed[:, :channels, :]
    bias_grad = packed[:, channels, :channels]
    return (ending[None], adjoint[None], weight_grad, bias_grad)


def solution(mesh):
    return jax.shard_map(
        per_device,
        mesh=mesh,
        in_specs=(
            P("batch", None, None),
            P("batch", None, None),
            P("layer", None, None),
            P("layer", None),
            P("layer", None),
            P("layer", None),
        ),
        out_specs=(
            P("layer", "batch", None, None),
            P("layer", "batch", None, None),
            P("layer", None, None),
            P("layer", None),
        ),
        check_vma=False,
    )
```

```python
import jax
import jax.numpy as jnp
from jax import lax
from jax.sharding import PartitionSpec as P

HEIGHT = 16
WIDTH = 32
ITERS = 2


step_size = 0.25


def columns(current):
    rounded = current.astype(jnp.bfloat16)
    pixels = HEIGHT * WIDTH
    margin = WIDTH + 1
    padded = jnp.pad(rounded, ((0, 0), (0, 0), (margin, margin)))
    across = jnp.arange(pixels) % WIDTH
    pieces = []
    for offset_y in (-1, 0, 1):
        for offset_x in (-1, 0, 1):
            shift_by = offset_y * WIDTH + offset_x
            inside = (across + offset_x >= 0) & (across + offset_x < WIDTH)
            window = padded[:, :, margin + shift_by : margin + shift_by + pixels]
            pieces.append(jnp.where(inside, window, jnp.zeros_like(window)))
    return jnp.concatenate(pieces, axis=1)


def flip_weight(weight):
    channels = weight.shape[0]
    taps = weight.reshape(channels, 9, channels)[:, ::-1, :]
    return jnp.transpose(taps, (2, 1, 0)).reshape(channels, 9 * channels)


def forward_layer(current, weight, bias_row):
    stacked = columns(current)
    pre_act = (
        jnp.einsum("ok,bkp->bop", weight, stacked, preferred_element_type=jnp.float32)
        + bias_row[None, :, None]
    )
    activity = jnp.tanh(pre_act)
    return (current + step_size * activity, activity, stacked)


def backward_layer(adjoint, activity, flipped):
    scaled = step_size * (1.0 - activity * activity) * adjoint
    rounded = scaled.astype(jnp.bfloat16)
    gathered = columns(rounded)
    back = jnp.einsum("ck,bkp->bcp", flipped, gathered, preferred_element_type=jnp.float32)
    return (adjoint + back, rounded, scaled)


def relax_block(start, weights, biases):
    current = start
    stored = []
    for layer_index in range(weights.shape[0]):
        current, activity, stacked = forward_layer(
            current, weights[layer_index], biases[layer_index]
        )
        stored.append((stacked, activity))
    return (current, stored)


def adjoint_block(finish, stored, flipped_list):
    adjoint = finish
    for layer_index in range(len(stored) - 1, -1, -1):
        adjoint = backward_layer(adjoint, stored[layer_index][1], flipped_list[layer_index])[0]
    return adjoint


def scan_distances(count):
    distances = []
    d = 1
    while d < count:
        distances.append(d)
        d *= 2
    return distances


def scan_pairs(count, d, reverse):
    if reverse:
        return [(k, k - d) for k in range(d, count)]
    return [(k, k + d) for k in range(count - d)]


def exclusive_scan_first(gain, local, axis, reverse):
    count = lax.axis_size(axis)
    channels, pixels = local.shape[1], local.shape[2]
    total = jnp.zeros_like(local)
    product = jnp.ones_like(gain)
    factors = []
    for d in scan_distances(count):
        sending = gain[None, :, None] * total + local
        gain_row = jnp.pad(gain * product, (0, pixels - channels))
        packed = jnp.concatenate([sending, gain_row[None, None, :]], axis=1)
        received = lax.ppermute(packed, axis, scan_pairs(count, d, reverse))
        factors.append(product)
        total = total + product[None, :, None] * received[:, :channels, :]
        product = product * received[0, channels, :channels]
    return total, factors


def exclusive_scan_again(gain, local, factors, axis, reverse):
    count = lax.axis_size(axis)
    total = jnp.zeros_like(local)
    for d, factor in zip(scan_distances(count), factors):
        sending = gain[None, :, None] * total + local
        received = lax.ppermute(sending, axis, scan_pairs(count, d, reverse))
        total = total + factor[None, :, None] * received
    return total


def batch_sum(value, axis):
    count = lax.axis_size(axis)
    me = lax.axis_index(axis)
    shape = value.shape
    flat = value.reshape(-1)
    lanes = 128
    quantum = lanes * 8 * count
    padded_size = -(-flat.shape[0] // quantum) * quantum
    current = jnp.pad(flat, (0, padded_size - flat.shape[0])).reshape(-1, lanes)
    steps = []
    step = 1
    while step < count:
        steps.append(step)
        step *= 2
    for step in steps:
        rows = current.shape[0] // 2
        mine = (me // step) % 2
        keep = lax.dynamic_slice_in_dim(current, mine * rows, rows, 0)
        give = lax.dynamic_slice_in_dim(current, (1 - mine) * rows, rows, 0)
        pairs = [(k, k ^ step) for k in range(count)]
        current = keep + lax.ppermute(give, axis, pairs)
    for step in steps[::-1]:
        rows = current.shape[0]
        mine = (me // step) % 2
        pairs = [(k, k ^ step) for k in range(count)]
        other = lax.ppermute(current, axis, pairs)
        whole = jnp.zeros((2 * rows, lanes), current.dtype)
        whole = lax.dynamic_update_slice_in_dim(whole, current, mine * rows, 0)
        current = lax.dynamic_update_slice_in_dim(whole, other, (1 - mine) * rows, 0)
    return current.reshape(-1)[: flat.shape[0]].reshape(shape)


def per_device(initial_state, cotangent, conv_weight, conv_bias, block_gain, adjoint_gain):
    gain_row = block_gain[0]
    back_row = adjoint_gain[0]
    flipped_list = [
        flip_weight(conv_weight[layer_index]) for layer_index in range(conv_weight.shape[0])
    ]
    c_points = initial_state
    following = initial_state
    for sweep_index in range(ITERS):
        ending = relax_block(c_points, conv_weight, conv_bias)[0]
        residual = ending - following
        if sweep_index == 0:
            error, factors = exclusive_scan_first(gain_row, residual, "layer", False)
        else:
            error = exclusive_scan_again(gain_row, residual, factors, "layer", False)
        c_points = c_points + error
        following = following + gain_row[None, :, None] * error + residual
    ending, stored = relax_block(c_points, conv_weight, conv_bias)
    target = cotangent
    previous = cotangent
    for sweep_index in range(ITERS):
        start_adj = adjoint_block(target, stored, flipped_list)
        residual = start_adj - previous
        if sweep_index == 0:
            error, factors = exclusive_scan_first(back_row, residual, "layer", True)
        else:
            error = exclusive_scan_again(back_row, residual, factors, "layer", True)
        target = target + error
        previous = previous + back_row[None, :, None] * error + residual
    adjoint = target
    weight_parts = []
    bias_parts = []
    for layer_index in range(len(stored) - 1, -1, -1):
        adjoint, rounded, scaled = backward_layer(
            adjoint, stored[layer_index][1], flipped_list[layer_index]
        )
        weight_part = jnp.einsum(
            "bop,bkp->ok", rounded, stored[layer_index][0], preferred_element_type=jnp.float32
        )
        bias_part = jnp.sum(scaled, axis=(0, 2))
        weight_parts.insert(0, weight_part)
        bias_parts.insert(0, bias_part)
    width = weight_parts[0].shape[1]
    channels = weight_parts[0].shape[0]
    packed = jnp.stack(
        [
            jnp.concatenate([w, jnp.pad(b, (0, width - channels))[None, :]], axis=0)
            for w, b in zip(weight_parts, bias_parts)
        ]
    )
    packed = batch_sum(packed, "batch")
    weight_grad = packed[:, :channels, :]
    bias_grad = packed[:, channels, :channels]
    return (ending[None], adjoint[None], weight_grad, bias_grad)


def solution(mesh):
    return jax.shard_map(
        per_device,
        mesh=mesh,
        in_specs=(
            P("batch", None, None),
            P("batch", None, None),
            P("layer", None, None),
            P("layer", None),
            P("layer", None),
            P("layer", None),
        ),
        out_specs=(
            P("layer", "batch", None, None),
            P("layer", "batch", None, None),
            P("layer", None, None),
            P("layer", None),
        ),
        check_vma=False,
    )
```

```python
import jax
import jax.numpy as jnp
from jax import lax
from jax.sharding import PartitionSpec as P

HEIGHT = 16
WIDTH = 32
ITERS = 2


step_size = 0.25


def columns(current):
    rounded = current.astype(jnp.bfloat16)
    pixels = HEIGHT * WIDTH
    margin = WIDTH + 1
    padded = jnp.pad(rounded, ((0, 0), (0, 0), (margin, margin)))
    across = jnp.arange(pixels) % WIDTH
    pieces = []
    for offset_y in (-1, 0, 1):
        for offset_x in (-1, 0, 1):
            shift_by = offset_y * WIDTH + offset_x
            inside = (across + offset_x >= 0) & (across + offset_x < WIDTH)
            window = padded[:, :, margin + shift_by : margin + shift_by + pixels]
            pieces.append(jnp.where(inside, window, jnp.zeros_like(window)))
    return jnp.concatenate(pieces, axis=1)


def flip_weight(weight):
    channels = weight.shape[0]
    taps = weight.reshape(channels, 9, channels)[:, ::-1, :]
    return jnp.transpose(taps, (2, 1, 0)).reshape(channels, 9 * channels)


def forward_layer(current, weight, bias_row):
    stacked = columns(current)
    pre_act = (
        jnp.einsum("ok,bkp->bop", weight, stacked, preferred_element_type=jnp.float32)
        + bias_row[None, :, None]
    )
    activity = jnp.tanh(pre_act)
    return (current + step_size * activity, activity, stacked)


def backward_layer(adjoint, activity, flipped):
    scaled = step_size * (1.0 - activity * activity) * adjoint
    rounded = scaled.astype(jnp.bfloat16)
    gathered = columns(rounded)
    back = jnp.einsum("ck,bkp->bcp", flipped, gathered, preferred_element_type=jnp.float32)
    return (adjoint + back, rounded, scaled)


def relax_block(start, weights, biases):
    current = start
    stored = []
    for layer_index in range(weights.shape[0]):
        current, activity, stacked = forward_layer(
            current, weights[layer_index], biases[layer_index]
        )
        stored.append((stacked, activity))
    return (current, stored)


def adjoint_block(finish, stored, flipped_list):
    adjoint = finish
    for layer_index in range(len(stored) - 1, -1, -1):
        adjoint = backward_layer(adjoint, stored[layer_index][1], flipped_list[layer_index])[0]
    return adjoint


def scan_distances(count):
    distances = []
    d = 1
    while d < count:
        distances.append(d)
        d *= 2
    return distances


def scan_pairs(count, d, reverse):
    if reverse:
        return [(k, k - d) for k in range(d, count)]
    return [(k, k + d) for k in range(count - d)]


def exclusive_scan_first(gain, local, axis, reverse):
    count = lax.axis_size(axis)
    channels, pixels = local.shape[1], local.shape[2]
    total = jnp.zeros_like(local)
    product = jnp.ones_like(gain)
    factors = []
    for d in scan_distances(count):
        sending = gain[None, :, None] * total + local
        gain_row = jnp.pad(gain * product, (0, pixels - channels))
        packed = jnp.concatenate([sending, gain_row[None, None, :]], axis=1)
        received = lax.ppermute(packed, axis, scan_pairs(count, d, reverse))
        factors.append(product)
        total = total + product[None, :, None] * received[:, :channels, :]
        product = product * received[0, channels, :channels]
    return total, factors


def exclusive_scan_again(gain, local, factors, axis, reverse):
    count = lax.axis_size(axis)
    total = jnp.zeros_like(local)
    for d, factor in zip(scan_distances(count), factors):
        sending = gain[None, :, None] * total + local
        received = lax.ppermute(sending, axis, scan_pairs(count, d, reverse))
        total = total + factor[None, :, None] * received
    return total


def batch_sum(value, axis):
    count = lax.axis_size(axis)
    chips = count // 2
    me = lax.axis_index(axis)
    core = me % 2
    chip = me // 2
    shape = value.shape
    flat = value.reshape(-1)
    lanes = 128
    quantum = lanes * 8 * count
    padded_size = -(-flat.shape[0] // quantum) * quantum
    current = jnp.pad(flat, (0, padded_size - flat.shape[0])).reshape(-1, lanes)
    half_rows = current.shape[0] // 2
    partner = [(k, k ^ 1) for k in range(count)]
    keep = lax.dynamic_slice_in_dim(current, core * half_rows, half_rows, 0)
    give = lax.dynamic_slice_in_dim(current, (1 - core) * half_rows, half_rows, 0)
    half = keep + lax.ppermute(give, axis, partner)

    def following(k):
        step = 1 if k % 2 == 0 else -1
        return ((k // 2 + step) % chips) * 2 + k % 2

    ring = [(k, following(k)) for k in range(count)]
    place = jnp.where(core == 0, chip, (chips - chip) % chips)
    pieces = half.reshape(chips, half_rows // chips, lanes)
    for t in range(chips - 1):
        sent = lax.dynamic_index_in_dim(pieces, (place - t) % chips, 0, False)
        got = lax.ppermute(sent, axis, ring)
        slot = (place - t - 1 + chips) % chips
        mine = lax.dynamic_index_in_dim(pieces, slot, 0, False)
        pieces = lax.dynamic_update_index_in_dim(pieces, mine + got, slot, 0)
    for t in range(chips - 1):
        sent = lax.dynamic_index_in_dim(pieces, (place + 1 - t + chips) % chips, 0, False)
        got = lax.ppermute(sent, axis, ring)
        pieces = lax.dynamic_update_index_in_dim(pieces, got, (place - t + chips) % chips, 0)
    half = pieces.reshape(half_rows, lanes)
    other = lax.ppermute(half, axis, partner)
    whole = jnp.zeros_like(current)
    whole = lax.dynamic_update_slice_in_dim(whole, half, core * half_rows, 0)
    whole = lax.dynamic_update_slice_in_dim(whole, other, (1 - core) * half_rows, 0)
    return whole.reshape(-1)[: flat.shape[0]].reshape(shape)


def per_device(initial_state, cotangent, conv_weight, conv_bias, block_gain, adjoint_gain):
    gain_row = block_gain[0]
    back_row = adjoint_gain[0]
    flipped_list = [
        flip_weight(conv_weight[layer_index]) for layer_index in range(conv_weight.shape[0])
    ]
    c_points = initial_state
    following = initial_state
    for sweep_index in range(ITERS):
        ending = relax_block(c_points, conv_weight, conv_bias)[0]
        residual = ending - following
        if sweep_index == 0:
            error, factors = exclusive_scan_first(gain_row, residual, "layer", False)
        else:
            error = exclusive_scan_again(gain_row, residual, factors, "layer", False)
        c_points = c_points + error
        following = following + gain_row[None, :, None] * error + residual
    ending, stored = relax_block(c_points, conv_weight, conv_bias)
    target = cotangent
    previous = cotangent
    for sweep_index in range(ITERS):
        start_adj = adjoint_block(target, stored, flipped_list)
        residual = start_adj - previous
        if sweep_index == 0:
            error, factors = exclusive_scan_first(back_row, residual, "layer", True)
        else:
            error = exclusive_scan_again(back_row, residual, factors, "layer", True)
        target = target + error
        previous = previous + back_row[None, :, None] * error + residual
    adjoint = target
    weight_parts = []
    bias_parts = []
    for layer_index in range(len(stored) - 1, -1, -1):
        adjoint, rounded, scaled = backward_layer(
            adjoint, stored[layer_index][1], flipped_list[layer_index]
        )
        weight_part = jnp.einsum(
            "bop,bkp->ok", rounded, stored[layer_index][0], preferred_element_type=jnp.float32
        )
        bias_part = jnp.sum(scaled, axis=(0, 2))
        weight_parts.insert(0, weight_part)
        bias_parts.insert(0, bias_part)
    width = weight_parts[0].shape[1]
    channels = weight_parts[0].shape[0]
    packed = jnp.stack(
        [
            jnp.concatenate([w, jnp.pad(b, (0, width - channels))[None, :]], axis=0)
            for w, b in zip(weight_parts, bias_parts)
        ]
    )
    packed = batch_sum(packed, "batch")
    weight_grad = packed[:, :channels, :]
    bias_grad = packed[:, channels, :channels]
    return (ending[None], adjoint[None], weight_grad, bias_grad)


def solution(mesh):
    return jax.shard_map(
        per_device,
        mesh=mesh,
        in_specs=(
            P("batch", None, None),
            P("batch", None, None),
            P("layer", None, None),
            P("layer", None),
            P("layer", None),
            P("layer", None),
        ),
        out_specs=(
            P("layer", "batch", None, None),
            P("layer", "batch", None, None),
            P("layer", None, None),
            P("layer", None),
        ),
        check_vma=False,
    )
```

```python
import jax
import jax.numpy as jnp
from jax import lax
from jax.sharding import PartitionSpec as P

HEIGHT = 16
WIDTH = 32
ITERS = 2


step_size = 0.25


def columns(current):
    rounded = current.astype(jnp.bfloat16)
    pixels = HEIGHT * WIDTH
    margin = WIDTH + 1
    padded = jnp.pad(rounded, ((0, 0), (0, 0), (margin, margin)))
    across = jnp.arange(pixels) % WIDTH
    pieces = []
    for offset_y in (-1, 0, 1):
        for offset_x in (-1, 0, 1):
            shift_by = offset_y * WIDTH + offset_x
            inside = (across + offset_x >= 0) & (across + offset_x < WIDTH)
            window = padded[:, :, margin + shift_by : margin + shift_by + pixels]
            pieces.append(jnp.where(inside, window, jnp.zeros_like(window)))
    return jnp.concatenate(pieces, axis=1)


def flip_weight(weight):
    channels = weight.shape[0]
    taps = weight.reshape(channels, 9, channels)[:, ::-1, :]
    return jnp.transpose(taps, (2, 1, 0)).reshape(channels, 9 * channels)


def forward_layer(current, weight, bias_row):
    stacked = columns(current)
    pre_act = (
        jnp.einsum("ok,bkp->bop", weight, stacked, preferred_element_type=jnp.float32)
        + bias_row[None, :, None]
    )
    activity = jnp.tanh(pre_act)
    return (current + step_size * activity, activity, stacked)


def backward_layer(adjoint, activity, flipped):
    scaled = step_size * (1.0 - activity * activity) * adjoint
    rounded = scaled.astype(jnp.bfloat16)
    gathered = columns(rounded)
    back = jnp.einsum("ck,bkp->bcp", flipped, gathered, preferred_element_type=jnp.float32)
    return (adjoint + back, rounded, scaled)


def relax_block(start, weights, biases):
    current = start
    stored = []
    for layer_index in range(weights.shape[0]):
        current, activity, stacked = forward_layer(
            current, weights[layer_index], biases[layer_index]
        )
        stored.append((stacked, activity))
    return (current, stored)


def adjoint_block(finish, stored, flipped_list):
    adjoint = finish
    for layer_index in range(len(stored) - 1, -1, -1):
        adjoint = backward_layer(adjoint, stored[layer_index][1], flipped_list[layer_index])[0]
    return adjoint


def scan_rounds(count):
    rounds = []
    d = 1
    while d < count:
        m = 3 if count % (4 * d) == 0 and d in (1, count // 4) else 1
        rounds.append((d, m))
        d *= m + 1
    return rounds


def scan_pairs(count, d, reverse):
    if reverse:
        return [(k, k - d) for k in range(d, count)]
    return [(k, k + d) for k in range(count - d)]


def exclusive_scan_first(gain, local, axis, reverse):
    count = lax.axis_size(axis)
    channels, pixels = local.shape[1], local.shape[2]
    total = jnp.zeros_like(local)
    product = jnp.ones_like(gain)
    factors = []
    for d, m in scan_rounds(count):
        sending = gain[None, :, None] * total + local
        gain_row = jnp.pad(gain * product, (0, pixels - channels))
        packed = jnp.concatenate([sending, gain_row[None, None, :]], axis=1)
        received = [
            lax.ppermute(packed, axis, scan_pairs(count, j * d, reverse)) for j in range(1, m + 1)
        ]
        for part in received:
            factors.append(product)
            total = total + product[None, :, None] * part[:, :channels, :]
            product = product * part[0, channels, :channels]
    return total, factors


def exclusive_scan_again(gain, local, factors, axis, reverse):
    count = lax.axis_size(axis)
    total = jnp.zeros_like(local)
    used = 0
    for d, m in scan_rounds(count):
        sending = gain[None, :, None] * total + local
        received = [
            lax.ppermute(sending, axis, scan_pairs(count, j * d, reverse)) for j in range(1, m + 1)
        ]
        for part in received:
            total = total + factors[used][None, :, None] * part
            used += 1
    return total


def batch_sum(value, axis):
    count = lax.axis_size(axis)
    chips = count // 2
    me = lax.axis_index(axis)
    core = me % 2
    chip = me // 2
    shape = value.shape
    flat = value.reshape(-1)
    lanes = 128
    quantum = lanes * 8 * count
    padded_size = -(-flat.shape[0] // quantum) * quantum
    current = jnp.pad(flat, (0, padded_size - flat.shape[0])).reshape(-1, lanes)
    half_rows = current.shape[0] // 2
    partner = [(k, k ^ 1) for k in range(count)]
    keep = lax.dynamic_slice_in_dim(current, core * half_rows, half_rows, 0)
    give = lax.dynamic_slice_in_dim(current, (1 - core) * half_rows, half_rows, 0)
    half = keep + lax.ppermute(give, axis, partner)

    def following(k):
        step = 1 if k % 2 == 0 else -1
        return ((k // 2 + step) % chips) * 2 + k % 2

    ring = [(k, following(k)) for k in range(count)]
    place = jnp.where(core == 0, chip, (chips - chip) % chips)
    pieces = half.reshape(chips, half_rows // chips, lanes)
    for t in range(chips - 1):
        sent = lax.dynamic_index_in_dim(pieces, (place - t) % chips, 0, False)
        got = lax.ppermute(sent, axis, ring)
        slot = (place - t - 1 + chips) % chips
        mine = lax.dynamic_index_in_dim(pieces, slot, 0, False)
        pieces = lax.dynamic_update_index_in_dim(pieces, mine + got, slot, 0)
    for t in range(chips - 1):
        sent = lax.dynamic_index_in_dim(pieces, (place + 1 - t + chips) % chips, 0, False)
        got = lax.ppermute(sent, axis, ring)
        pieces = lax.dynamic_update_index_in_dim(pieces, got, (place - t + chips) % chips, 0)
    half = pieces.reshape(half_rows, lanes)
    other = lax.ppermute(half, axis, partner)
    whole = jnp.zeros_like(current)
    whole = lax.dynamic_update_slice_in_dim(whole, half, core * half_rows, 0)
    whole = lax.dynamic_update_slice_in_dim(whole, other, (1 - core) * half_rows, 0)
    return whole.reshape(-1)[: flat.shape[0]].reshape(shape)


def per_device(initial_state, cotangent, conv_weight, conv_bias, block_gain, adjoint_gain):
    gain_row = block_gain[0]
    back_row = adjoint_gain[0]
    flipped_list = [
        flip_weight(conv_weight[layer_index]) for layer_index in range(conv_weight.shape[0])
    ]
    c_points = initial_state
    following = initial_state
    for sweep_index in range(ITERS):
        ending = relax_block(c_points, conv_weight, conv_bias)[0]
        residual = ending - following
        if sweep_index == 0:
            error, factors = exclusive_scan_first(gain_row, residual, "layer", False)
        else:
            error = exclusive_scan_again(gain_row, residual, factors, "layer", False)
        c_points = c_points + error
        following = following + gain_row[None, :, None] * error + residual
    ending, stored = relax_block(c_points, conv_weight, conv_bias)
    target = cotangent
    previous = cotangent
    for sweep_index in range(ITERS):
        start_adj = adjoint_block(target, stored, flipped_list)
        residual = start_adj - previous
        if sweep_index == 0:
            error, factors = exclusive_scan_first(back_row, residual, "layer", True)
        else:
            error = exclusive_scan_again(back_row, residual, factors, "layer", True)
        target = target + error
        previous = previous + back_row[None, :, None] * error + residual
    adjoint = target
    weight_parts = []
    bias_parts = []
    for layer_index in range(len(stored) - 1, -1, -1):
        adjoint, rounded, scaled = backward_layer(
            adjoint, stored[layer_index][1], flipped_list[layer_index]
        )
        weight_part = jnp.einsum(
            "bop,bkp->ok", rounded, stored[layer_index][0], preferred_element_type=jnp.float32
        )
        bias_part = jnp.sum(scaled, axis=(0, 2))
        weight_parts.insert(0, weight_part)
        bias_parts.insert(0, bias_part)
    width = weight_parts[0].shape[1]
    channels = weight_parts[0].shape[0]
    packed = jnp.stack(
        [
            jnp.concatenate([w, jnp.pad(b, (0, width - channels))[None, :]], axis=0)
            for w, b in zip(weight_parts, bias_parts)
        ]
    )
    packed = batch_sum(packed, "batch")
    weight_grad = packed[:, :channels, :]
    bias_grad = packed[:, channels, :channels]
    return (ending[None], adjoint[None], weight_grad, bias_grad)


def solution(mesh):
    return jax.shard_map(
        per_device,
        mesh=mesh,
        in_specs=(
            P("batch", None, None),
            P("batch", None, None),
            P("layer", None, None),
            P("layer", None),
            P("layer", None),
            P("layer", None),
        ),
        out_specs=(
            P("layer", "batch", None, None),
            P("layer", "batch", None, None),
            P("layer", None, None),
            P("layer", None),
        ),
        check_vma=False,
    )
```

```python
import jax
import jax.numpy as jnp
from jax import lax
from jax.sharding import PartitionSpec as P

HEIGHT = 16
WIDTH = 32
ITERS = 2


step_size = 0.25


def columns(current):
    rounded = current.astype(jnp.bfloat16)
    pixels = HEIGHT * WIDTH
    margin = WIDTH + 1
    padded = jnp.pad(rounded, ((0, 0), (0, 0), (margin, margin)))
    across = jnp.arange(pixels) % WIDTH
    pieces = []
    for offset_y in (-1, 0, 1):
        for offset_x in (-1, 0, 1):
            shift_by = offset_y * WIDTH + offset_x
            inside = (across + offset_x >= 0) & (across + offset_x < WIDTH)
            window = padded[:, :, margin + shift_by : margin + shift_by + pixels]
            pieces.append(jnp.where(inside, window, jnp.zeros_like(window)))
    return jnp.concatenate(pieces, axis=1)


def flip_weight(weight):
    channels = weight.shape[0]
    taps = weight.reshape(channels, 9, channels)[:, ::-1, :]
    return jnp.transpose(taps, (2, 1, 0)).reshape(channels, 9 * channels)


def forward_layer(current, weight, bias_row):
    stacked = columns(current)
    pre_act = (
        jnp.einsum("ok,bkp->bop", weight, stacked, preferred_element_type=jnp.float32)
        + bias_row[None, :, None]
    )
    activity = jnp.tanh(pre_act)
    return (current + step_size * activity, activity, stacked)


def backward_layer(adjoint, activity, flipped):
    scaled = step_size * (1.0 - activity * activity) * adjoint
    rounded = scaled.astype(jnp.bfloat16)
    gathered = columns(rounded)
    back = jnp.einsum("ck,bkp->bcp", flipped, gathered, preferred_element_type=jnp.float32)
    return (adjoint + back, rounded, scaled)


def relax_block(start, weights, biases):
    current = start
    stored = []
    for layer_index in range(weights.shape[0]):
        current, activity, stacked = forward_layer(
            current, weights[layer_index], biases[layer_index]
        )
        stored.append((stacked, activity))
    return (current, stored)


def adjoint_block(finish, stored, flipped_list):
    adjoint = finish
    for layer_index in range(len(stored) - 1, -1, -1):
        adjoint = backward_layer(adjoint, stored[layer_index][1], flipped_list[layer_index])[0]
    return adjoint


def scan_rounds(count):
    rounds = []
    d = 1
    while d < count:
        m = 3 if count % (4 * d) == 0 and d in (1, count // 4) else 1
        rounds.append((d, m))
        d *= m + 1
    return rounds


def scan_pairs(count, d, reverse):
    if reverse:
        return [(k, k - d) for k in range(d, count)]
    return [(k, k + d) for k in range(count - d)]


def exclusive_scan_first(gain, local, axis, reverse):
    count = lax.axis_size(axis)
    channels, pixels = local.shape[1], local.shape[2]
    total = jnp.zeros_like(local)
    product = jnp.ones_like(gain)
    factors = []
    for d, m in scan_rounds(count):
        sending = gain[None, :, None] * total + local
        gain_row = jnp.pad(gain * product, (0, pixels - channels))
        packed = jnp.concatenate([sending, gain_row[None, None, :]], axis=1)
        received = [
            lax.ppermute(packed, axis, scan_pairs(count, j * d, reverse)) for j in range(1, m + 1)
        ]
        for part in received:
            factors.append(product)
            total = total + product[None, :, None] * part[:, :channels, :]
            product = product * part[0, channels, :channels]
    return total, factors


def exclusive_scan_again(gain, local, factors, axis, reverse):
    count = lax.axis_size(axis)
    total = jnp.zeros_like(local)
    used = 0
    for d, m in scan_rounds(count):
        sending = gain[None, :, None] * total + local
        received = [
            lax.ppermute(sending, axis, scan_pairs(count, j * d, reverse)) for j in range(1, m + 1)
        ]
        for part in received:
            total = total + factors[used][None, :, None] * part
            used += 1
    return total


def batch_sum(value, axis):
    count = lax.axis_size(axis)
    chips = count // 2
    me = lax.axis_index(axis)
    core = me % 2
    chip = me // 2
    shape = value.shape
    flat = value.reshape(-1)
    lanes = 128
    quantum = lanes * 8 * count
    padded_size = -(-flat.shape[0] // quantum) * quantum
    current = jnp.pad(flat, (0, padded_size - flat.shape[0])).reshape(-1, lanes)
    half_rows = current.shape[0] // 2
    partner = [(k, k ^ 1) for k in range(count)]
    keep = lax.dynamic_slice_in_dim(current, core * half_rows, half_rows, 0)
    give = lax.dynamic_slice_in_dim(current, (1 - core) * half_rows, half_rows, 0)
    half = keep + lax.ppermute(give, axis, partner)

    pieces = half.reshape(chips, half_rows // chips, lanes)
    mine = lax.dynamic_index_in_dim(pieces, chip, 0, False)
    for shift in range(1, chips):
        target = [(k, ((k // 2 + shift) % chips) * 2 + k % 2) for k in range(count)]
        sent = lax.dynamic_index_in_dim(pieces, (chip + shift) % chips, 0, False)
        mine = mine + lax.ppermute(sent, axis, target)
    pieces = lax.dynamic_update_index_in_dim(pieces, mine, chip, 0)
    for shift in range(1, chips):
        target = [(k, ((k // 2 + shift) % chips) * 2 + k % 2) for k in range(count)]
        got = lax.ppermute(mine, axis, target)
        pieces = lax.dynamic_update_index_in_dim(pieces, got, (chip - shift + chips) % chips, 0)
    half = pieces.reshape(half_rows, lanes)
    other = lax.ppermute(half, axis, partner)
    whole = jnp.zeros_like(current)
    whole = lax.dynamic_update_slice_in_dim(whole, half, core * half_rows, 0)
    whole = lax.dynamic_update_slice_in_dim(whole, other, (1 - core) * half_rows, 0)
    return whole.reshape(-1)[: flat.shape[0]].reshape(shape)


def per_device(initial_state, cotangent, conv_weight, conv_bias, block_gain, adjoint_gain):
    gain_row = block_gain[0]
    back_row = adjoint_gain[0]
    flipped_list = [
        flip_weight(conv_weight[layer_index]) for layer_index in range(conv_weight.shape[0])
    ]
    c_points = initial_state
    following = initial_state
    for sweep_index in range(ITERS):
        ending = relax_block(c_points, conv_weight, conv_bias)[0]
        residual = ending - following
        if sweep_index == 0:
            error, factors = exclusive_scan_first(gain_row, residual, "layer", False)
        else:
            error = exclusive_scan_again(gain_row, residual, factors, "layer", False)
        c_points = c_points + error
        following = following + gain_row[None, :, None] * error + residual
    ending, stored = relax_block(c_points, conv_weight, conv_bias)
    target = cotangent
    previous = cotangent
    for sweep_index in range(ITERS):
        start_adj = adjoint_block(target, stored, flipped_list)
        residual = start_adj - previous
        if sweep_index == 0:
            error, factors = exclusive_scan_first(back_row, residual, "layer", True)
        else:
            error = exclusive_scan_again(back_row, residual, factors, "layer", True)
        target = target + error
        previous = previous + back_row[None, :, None] * error + residual
    adjoint = target
    weight_parts = []
    bias_parts = []
    for layer_index in range(len(stored) - 1, -1, -1):
        adjoint, rounded, scaled = backward_layer(
            adjoint, stored[layer_index][1], flipped_list[layer_index]
        )
        weight_part = jnp.einsum(
            "bop,bkp->ok", rounded, stored[layer_index][0], preferred_element_type=jnp.float32
        )
        bias_part = jnp.sum(scaled, axis=(0, 2))
        weight_parts.insert(0, weight_part)
        bias_parts.insert(0, bias_part)
    width = weight_parts[0].shape[1]
    channels = weight_parts[0].shape[0]
    packed = jnp.stack(
        [
            jnp.concatenate([w, jnp.pad(b, (0, width - channels))[None, :]], axis=0)
            for w, b in zip(weight_parts, bias_parts)
        ]
    )
    packed = batch_sum(packed, "batch")
    weight_grad = packed[:, :channels, :]
    bias_grad = packed[:, channels, :channels]
    return (ending[None], adjoint[None], weight_grad, bias_grad)


def solution(mesh):
    return jax.shard_map(
        per_device,
        mesh=mesh,
        in_specs=(
            P("batch", None, None),
            P("batch", None, None),
            P("layer", None, None),
            P("layer", None),
            P("layer", None),
            P("layer", None),
        ),
        out_specs=(
            P("layer", "batch", None, None),
            P("layer", "batch", None, None),
            P("layer", None, None),
            P("layer", None),
        ),
        check_vma=False,
    )
```

```python
import jax
import jax.numpy as jnp
from jax import lax
from jax.sharding import PartitionSpec as P

HEIGHT = 16
WIDTH = 32
ITERS = 2


step_size = 0.25


def columns(current):
    rounded = current.astype(jnp.bfloat16)
    pixels = HEIGHT * WIDTH
    margin = WIDTH + 1
    padded = jnp.pad(rounded, ((0, 0), (0, 0), (margin, margin)))
    across = jnp.arange(pixels) % WIDTH
    pieces = []
    for offset_y in (-1, 0, 1):
        for offset_x in (-1, 0, 1):
            shift_by = offset_y * WIDTH + offset_x
            inside = (across + offset_x >= 0) & (across + offset_x < WIDTH)
            window = padded[:, :, margin + shift_by : margin + shift_by + pixels]
            pieces.append(jnp.where(inside, window, jnp.zeros_like(window)))
    return jnp.concatenate(pieces, axis=1)


def flip_weight(weight):
    channels = weight.shape[0]
    taps = weight.reshape(channels, 9, channels)[:, ::-1, :]
    return jnp.transpose(taps, (2, 1, 0)).reshape(channels, 9 * channels)


def conv_same(current, kernel):
    batch, channels, pixels = current.shape
    image = current.astype(jnp.bfloat16).reshape(batch, channels, HEIGHT, WIDTH)
    out = lax.conv_general_dilated(
        image,
        jnp.transpose(kernel, (0, 3, 1, 2)),
        (1, 1),
        ((1, 1), (1, 1)),
        dimension_numbers=("NCHW", "OIHW", "NCHW"),
        preferred_element_type=jnp.float32,
    )
    return out.reshape(batch, kernel.shape[0], pixels)


def forward_layer(current, weight, bias_row):
    channels = weight.shape[0]
    pre_act = conv_same(current, weight.reshape(channels, 3, 3, channels)) + bias_row[None, :, None]
    activity = jnp.tanh(pre_act)
    return (current + step_size * activity, activity, current)


def backward_layer(adjoint, activity, flipped):
    scaled = step_size * (1.0 - activity * activity) * adjoint
    rounded = scaled.astype(jnp.bfloat16)
    channels = flipped.shape[0]
    back = conv_same(rounded, flipped.reshape(channels, 3, 3, channels))
    return (adjoint + back, rounded, scaled)


def relax_block(start, weights, biases):
    current = start
    stored = []
    for layer_index in range(weights.shape[0]):
        current, activity, stacked = forward_layer(
            current, weights[layer_index], biases[layer_index]
        )
        stored.append((stacked, activity))
    return (current, stored)


def adjoint_block(finish, stored, flipped_list):
    adjoint = finish
    for layer_index in range(len(stored) - 1, -1, -1):
        adjoint = backward_layer(adjoint, stored[layer_index][1], flipped_list[layer_index])[0]
    return adjoint


def scan_rounds(count):
    rounds = []
    d = 1
    while d < count:
        m = 3 if count % (4 * d) == 0 and d in (1, count // 4) else 1
        rounds.append((d, m))
        d *= m + 1
    return rounds


def scan_pairs(count, d, reverse):
    if reverse:
        return [(k, k - d) for k in range(d, count)]
    return [(k, k + d) for k in range(count - d)]


def exclusive_scan_first(gain, local, axis, reverse):
    count = lax.axis_size(axis)
    channels, pixels = local.shape[1], local.shape[2]
    total = jnp.zeros_like(local)
    product = jnp.ones_like(gain)
    factors = []
    for d, m in scan_rounds(count):
        sending = gain[None, :, None] * total + local
        gain_row = jnp.pad(gain * product, (0, pixels - channels))
        packed = jnp.concatenate([sending, gain_row[None, None, :]], axis=1)
        received = [
            lax.ppermute(packed, axis, scan_pairs(count, j * d, reverse)) for j in range(1, m + 1)
        ]
        for part in received:
            factors.append(product)
            total = total + product[None, :, None] * part[:, :channels, :]
            product = product * part[0, channels, :channels]
    return total, factors


def exclusive_scan_again(gain, local, factors, axis, reverse):
    count = lax.axis_size(axis)
    total = jnp.zeros_like(local)
    used = 0
    for d, m in scan_rounds(count):
        sending = gain[None, :, None] * total + local
        received = [
            lax.ppermute(sending, axis, scan_pairs(count, j * d, reverse)) for j in range(1, m + 1)
        ]
        for part in received:
            total = total + factors[used][None, :, None] * part
            used += 1
    return total


def batch_sum(value, axis):
    count = lax.axis_size(axis)
    chips = count // 2
    me = lax.axis_index(axis)
    core = me % 2
    chip = me // 2
    shape = value.shape
    flat = value.reshape(-1)
    lanes = 128
    quantum = lanes * 8 * count
    padded_size = -(-flat.shape[0] // quantum) * quantum
    current = jnp.pad(flat, (0, padded_size - flat.shape[0])).reshape(-1, lanes)
    half_rows = current.shape[0] // 2
    partner = [(k, k ^ 1) for k in range(count)]
    keep = lax.dynamic_slice_in_dim(current, core * half_rows, half_rows, 0)
    give = lax.dynamic_slice_in_dim(current, (1 - core) * half_rows, half_rows, 0)
    half = keep + lax.ppermute(give, axis, partner)

    pieces = half.reshape(chips, half_rows // chips, lanes)
    mine = lax.dynamic_index_in_dim(pieces, chip, 0, False)
    for shift in range(1, chips):
        target = [(k, ((k // 2 + shift) % chips) * 2 + k % 2) for k in range(count)]
        sent = lax.dynamic_index_in_dim(pieces, (chip + shift) % chips, 0, False)
        mine = mine + lax.ppermute(sent, axis, target)
    pieces = lax.dynamic_update_index_in_dim(pieces, mine, chip, 0)
    for shift in range(1, chips):
        target = [(k, ((k // 2 + shift) % chips) * 2 + k % 2) for k in range(count)]
        got = lax.ppermute(mine, axis, target)
        pieces = lax.dynamic_update_index_in_dim(pieces, got, (chip - shift + chips) % chips, 0)
    half = pieces.reshape(half_rows, lanes)
    other = lax.ppermute(half, axis, partner)
    whole = jnp.zeros_like(current)
    whole = lax.dynamic_update_slice_in_dim(whole, half, core * half_rows, 0)
    whole = lax.dynamic_update_slice_in_dim(whole, other, (1 - core) * half_rows, 0)
    return whole.reshape(-1)[: flat.shape[0]].reshape(shape)


def per_device(initial_state, cotangent, conv_weight, conv_bias, block_gain, adjoint_gain):
    gain_row = block_gain[0]
    back_row = adjoint_gain[0]
    flipped_list = [
        flip_weight(conv_weight[layer_index]) for layer_index in range(conv_weight.shape[0])
    ]
    c_points = initial_state
    following = initial_state
    for sweep_index in range(ITERS):
        ending = relax_block(c_points, conv_weight, conv_bias)[0]
        residual = ending - following
        if sweep_index == 0:
            error, factors = exclusive_scan_first(gain_row, residual, "layer", False)
        else:
            error = exclusive_scan_again(gain_row, residual, factors, "layer", False)
        c_points = c_points + error
        following = following + gain_row[None, :, None] * error + residual
    ending, stored = relax_block(c_points, conv_weight, conv_bias)
    target = cotangent
    previous = cotangent
    for sweep_index in range(ITERS):
        start_adj = adjoint_block(target, stored, flipped_list)
        residual = start_adj - previous
        if sweep_index == 0:
            error, factors = exclusive_scan_first(back_row, residual, "layer", True)
        else:
            error = exclusive_scan_again(back_row, residual, factors, "layer", True)
        target = target + error
        previous = previous + back_row[None, :, None] * error + residual
    adjoint = target
    weight_parts = []
    bias_parts = []
    for layer_index in range(len(stored) - 1, -1, -1):
        adjoint, rounded, scaled = backward_layer(
            adjoint, stored[layer_index][1], flipped_list[layer_index]
        )
        weight_part = jnp.einsum(
            "bop,bkp->ok", rounded, columns(stored[layer_index][0]), preferred_element_type=jnp.float32
        )
        bias_part = jnp.sum(scaled, axis=(0, 2))
        weight_parts.insert(0, weight_part)
        bias_parts.insert(0, bias_part)
    width = weight_parts[0].shape[1]
    channels = weight_parts[0].shape[0]
    packed = jnp.stack(
        [
            jnp.concatenate([w, jnp.pad(b, (0, width - channels))[None, :]], axis=0)
            for w, b in zip(weight_parts, bias_parts)
        ]
    )
    packed = batch_sum(packed, "batch")
    weight_grad = packed[:, :channels, :]
    bias_grad = packed[:, channels, :channels]
    return (ending[None], adjoint[None], weight_grad, bias_grad)


def solution(mesh):
    return jax.shard_map(
        per_device,
        mesh=mesh,
        in_specs=(
            P("batch", None, None),
            P("batch", None, None),
            P("layer", None, None),
            P("layer", None),
            P("layer", None),
            P("layer", None),
        ),
        out_specs=(
            P("layer", "batch", None, None),
            P("layer", "batch", None, None),
            P("layer", None, None),
            P("layer", None),
        ),
        check_vma=False,
    )
```

```python
import jax
import jax.numpy as jnp
from jax import lax
from jax.sharding import PartitionSpec as P

HEIGHT = 16
WIDTH = 32
ITERS = 2


step_size = 0.25


def columns(current):
    rounded = current.astype(jnp.bfloat16)
    pixels = HEIGHT * WIDTH
    margin = WIDTH + 1
    padded = jnp.pad(rounded, ((0, 0), (0, 0), (margin, margin)))
    across = jnp.arange(pixels) % WIDTH
    pieces = []
    for offset_y in (-1, 0, 1):
        for offset_x in (-1, 0, 1):
            shift_by = offset_y * WIDTH + offset_x
            inside = (across + offset_x >= 0) & (across + offset_x < WIDTH)
            window = padded[:, :, margin + shift_by : margin + shift_by + pixels]
            pieces.append(jnp.where(inside, window, jnp.zeros_like(window)))
    return jnp.concatenate(pieces, axis=1)


def shifted_sum(spread, inverse):
    pixels = HEIGHT * WIDTH
    margin = WIDTH + 1
    across = jnp.arange(pixels) % WIDTH
    summed = None
    tap_index = 0
    for offset_y in (-1, 0, 1):
        for offset_x in (-1, 0, 1):
            shift_by = offset_y * WIDTH + offset_x
            window = spread[:, tap_index]
            if inverse:
                inside = (across + offset_x >= 0) & (across + offset_x < WIDTH)
                masked = jnp.where(inside, window, jnp.zeros_like(window))
                placed = jnp.pad(masked, ((0, 0), (0, 0), (margin + shift_by, margin - shift_by)))
                piece = placed[:, :, margin : margin + pixels]
            else:
                padded = jnp.pad(window, ((0, 0), (0, 0), (margin, margin)))
                piece = padded[:, :, margin + shift_by : margin + shift_by + pixels]
                inside = (across + offset_x >= 0) & (across + offset_x < WIDTH)
                piece = jnp.where(inside, piece, jnp.zeros_like(piece))
            summed = piece if summed is None else summed + piece
            tap_index = tap_index + 1
    return summed


def forward_layer(current, weight, bias_row):
    channels = weight.shape[0]
    per_tap = jnp.transpose(weight.reshape(channels, 9, channels), (1, 0, 2))
    spread = jnp.einsum(
        "toc,bcp->btop", per_tap, current.astype(jnp.bfloat16), preferred_element_type=jnp.float32
    )
    pre_act = shifted_sum(spread, False) + bias_row[None, :, None]
    activity = jnp.tanh(pre_act)
    return (current + step_size * activity, activity, current)


def backward_layer(adjoint, activity, weight):
    scaled = step_size * (1.0 - activity * activity) * adjoint
    rounded = scaled.astype(jnp.bfloat16)
    channels = weight.shape[0]
    per_tap = weight.reshape(channels, 9, channels)
    spread = jnp.einsum("otc,bop->btcp", per_tap, rounded, preferred_element_type=jnp.float32)
    back = shifted_sum(spread, True)
    return (adjoint + back, rounded, scaled)


def relax_block(start, weights, biases):
    current = start
    stored = []
    for layer_index in range(weights.shape[0]):
        current, activity, stacked = forward_layer(
            current, weights[layer_index], biases[layer_index]
        )
        stored.append((stacked, activity))
    return (current, stored)


def adjoint_block(finish, stored, weight_list):
    adjoint = finish
    for layer_index in range(len(stored) - 1, -1, -1):
        adjoint = backward_layer(adjoint, stored[layer_index][1], weight_list[layer_index])[0]
    return adjoint


def scan_distances(count):
    distances = []
    d = 1
    while d < count:
        distances.append(d)
        d *= 2
    return distances


def scan_pairs(count, d, reverse):
    if reverse:
        return [(k, k - d) for k in range(d, count)]
    return [(k, k + d) for k in range(count - d)]


def exclusive_scan_first(gain, local, axis, reverse):
    count = lax.axis_size(axis)
    channels, pixels = local.shape[1], local.shape[2]
    total = jnp.zeros_like(local)
    product = jnp.ones_like(gain)
    factors = []
    for d in scan_distances(count):
        sending = gain[None, :, None] * total + local
        gain_row = jnp.pad(gain * product, (0, pixels - channels))
        packed = jnp.concatenate([sending, gain_row[None, None, :]], axis=1)
        received = lax.ppermute(packed, axis, scan_pairs(count, d, reverse))
        factors.append(product)
        total = total + product[None, :, None] * received[:, :channels, :]
        product = product * received[0, channels, :channels]
    return total, factors


def exclusive_scan_again(gain, local, factors, axis, reverse):
    count = lax.axis_size(axis)
    total = jnp.zeros_like(local)
    for d, factor in zip(scan_distances(count), factors):
        sending = gain[None, :, None] * total + local
        received = lax.ppermute(sending, axis, scan_pairs(count, d, reverse))
        total = total + factor[None, :, None] * received
    return total


def batch_sum(value, axis):
    count = lax.axis_size(axis)
    chips = count // 2
    me = lax.axis_index(axis)
    core = me % 2
    chip = me // 2
    shape = value.shape
    flat = value.reshape(-1)
    lanes = 128
    quantum = lanes * 8 * count
    padded_size = -(-flat.shape[0] // quantum) * quantum
    current = jnp.pad(flat, (0, padded_size - flat.shape[0])).reshape(-1, lanes)
    half_rows = current.shape[0] // 2
    partner = [(k, k ^ 1) for k in range(count)]
    keep = lax.dynamic_slice_in_dim(current, core * half_rows, half_rows, 0)
    give = lax.dynamic_slice_in_dim(current, (1 - core) * half_rows, half_rows, 0)
    half = keep + lax.ppermute(give, axis, partner)

    def following(k):
        step = 1 if k % 2 == 0 else -1
        return ((k // 2 + step) % chips) * 2 + k % 2

    ring = [(k, following(k)) for k in range(count)]
    place = jnp.where(core == 0, chip, (chips - chip) % chips)
    pieces = half.reshape(chips, half_rows // chips, lanes)
    for t in range(chips - 1):
        sent = lax.dynamic_index_in_dim(pieces, (place - t) % chips, 0, False)
        got = lax.ppermute(sent, axis, ring)
        slot = (place - t - 1 + chips) % chips
        mine = lax.dynamic_index_in_dim(pieces, slot, 0, False)
        pieces = lax.dynamic_update_index_in_dim(pieces, mine + got, slot, 0)
    for t in range(chips - 1):
        sent = lax.dynamic_index_in_dim(pieces, (place + 1 - t + chips) % chips, 0, False)
        got = lax.ppermute(sent, axis, ring)
        pieces = lax.dynamic_update_index_in_dim(pieces, got, (place - t + chips) % chips, 0)
    half = pieces.reshape(half_rows, lanes)
    other = lax.ppermute(half, axis, partner)
    whole = jnp.zeros_like(current)
    whole = lax.dynamic_update_slice_in_dim(whole, half, core * half_rows, 0)
    whole = lax.dynamic_update_slice_in_dim(whole, other, (1 - core) * half_rows, 0)
    return whole.reshape(-1)[: flat.shape[0]].reshape(shape)


def per_device(initial_state, cotangent, conv_weight, conv_bias, block_gain, adjoint_gain):
    gain_row = block_gain[0]
    back_row = adjoint_gain[0]
    weight_list = [conv_weight[layer_index] for layer_index in range(conv_weight.shape[0])]
    c_points = initial_state
    following = initial_state
    for sweep_index in range(ITERS):
        ending = relax_block(c_points, conv_weight, conv_bias)[0]
        residual = ending - following
        if sweep_index == 0:
            error, factors = exclusive_scan_first(gain_row, residual, "layer", False)
        else:
            error = exclusive_scan_again(gain_row, residual, factors, "layer", False)
        c_points = c_points + error
        following = following + gain_row[None, :, None] * error + residual
    ending, stored = relax_block(c_points, conv_weight, conv_bias)
    target = cotangent
    previous = cotangent
    for sweep_index in range(ITERS):
        start_adj = adjoint_block(target, stored, weight_list)
        residual = start_adj - previous
        if sweep_index == 0:
            error, factors = exclusive_scan_first(back_row, residual, "layer", True)
        else:
            error = exclusive_scan_again(back_row, residual, factors, "layer", True)
        target = target + error
        previous = previous + back_row[None, :, None] * error + residual
    adjoint = target
    weight_parts = []
    bias_parts = []
    for layer_index in range(len(stored) - 1, -1, -1):
        adjoint, rounded, scaled = backward_layer(
            adjoint, stored[layer_index][1], weight_list[layer_index]
        )
        weight_part = jnp.einsum(
            "bop,bkp->ok",
            rounded,
            columns(stored[layer_index][0]),
            preferred_element_type=jnp.float32,
        )
        bias_part = jnp.sum(scaled, axis=(0, 2))
        weight_parts.insert(0, weight_part)
        bias_parts.insert(0, bias_part)
    width = weight_parts[0].shape[1]
    channels = weight_parts[0].shape[0]
    packed = jnp.stack(
        [
            jnp.concatenate([w, jnp.pad(b, (0, width - channels))[None, :]], axis=0)
            for w, b in zip(weight_parts, bias_parts)
        ]
    )
    packed = batch_sum(packed, "batch")
    weight_grad = packed[:, :channels, :]
    bias_grad = packed[:, channels, :channels]
    return (ending[None], adjoint[None], weight_grad, bias_grad)


def solution(mesh):
    return jax.shard_map(
        per_device,
        mesh=mesh,
        in_specs=(
            P("batch", None, None),
            P("batch", None, None),
            P("layer", None, None),
            P("layer", None),
            P("layer", None),
            P("layer", None),
        ),
        out_specs=(
            P("layer", "batch", None, None),
            P("layer", "batch", None, None),
            P("layer", None, None),
            P("layer", None),
        ),
        check_vma=False,
    )
```

```python
import jax
import jax.numpy as jnp
from jax import lax
from jax.sharding import PartitionSpec as P

HEIGHT = 16
WIDTH = 32
ITERS = 2


step_size = 0.25


def columns(current):
    rounded = current.astype(jnp.bfloat16)
    pixels = HEIGHT * WIDTH
    margin = WIDTH + 1
    padded = jnp.pad(rounded, ((0, 0), (0, 0), (margin, margin)))
    across = jnp.arange(pixels) % WIDTH
    pieces = []
    for offset_y in (-1, 0, 1):
        for offset_x in (-1, 0, 1):
            shift_by = offset_y * WIDTH + offset_x
            inside = (across + offset_x >= 0) & (across + offset_x < WIDTH)
            window = padded[:, :, margin + shift_by : margin + shift_by + pixels]
            pieces.append(jnp.where(inside, window, jnp.zeros_like(window)))
    return jnp.concatenate(pieces, axis=1)


def flip_weight(weight):
    channels = weight.shape[0]
    taps = weight.reshape(channels, 9, channels)[:, ::-1, :]
    return jnp.transpose(taps, (2, 1, 0)).reshape(channels, 9 * channels)


def forward_layer(current, weight, bias_row):
    stacked = columns(current)
    pre_act = (
        jnp.einsum("ok,bkp->bop", weight, stacked, preferred_element_type=jnp.float32)
        + bias_row[None, :, None]
    )
    activity = jnp.tanh(pre_act)
    return (current + step_size * activity, activity, stacked)


def backward_layer(adjoint, activity, flipped):
    scaled = step_size * (1.0 - activity * activity) * adjoint
    rounded = scaled.astype(jnp.bfloat16)
    gathered = columns(rounded)
    back = jnp.einsum("ck,bkp->bcp", flipped, gathered, preferred_element_type=jnp.float32)
    return (adjoint + back, rounded, scaled)


def relax_block(start, weights, biases):
    current = start
    stored = []
    for layer_index in range(weights.shape[0]):
        current, activity, stacked = forward_layer(
            current, weights[layer_index], biases[layer_index]
        )
        stored.append((stacked, activity))
    return (current, stored)


def adjoint_block(finish, stored, flipped_list):
    adjoint = finish
    for layer_index in range(len(stored) - 1, -1, -1):
        adjoint = backward_layer(adjoint, stored[layer_index][1], flipped_list[layer_index])[0]
    return adjoint


def butterfly_first(gain, local, axis, reverse):
    count = lax.axis_size(axis)
    me = lax.axis_index(axis)
    place = count - 1 - me if reverse else me
    channels, pixels = local.shape[1], local.shape[2]
    total = jnp.zeros_like(local)
    product = jnp.ones_like(gain)
    block_sum = local
    block_gain = gain
    factors = []
    step = 1
    while step < count:
        upper = (place // step) % 2 == 1
        gain_row = jnp.pad(block_gain, (0, pixels - channels))
        packed = jnp.concatenate([block_sum, gain_row[None, None, :]], axis=1)
        got = lax.ppermute(packed, axis, [(k, k ^ step) for k in range(count)])
        other_sum = got[:, :channels, :]
        other_gain = got[0, channels, :channels]
        upper_gain = jnp.where(upper, block_gain, other_gain)
        factors.append((product, upper_gain))
        total = jnp.where(upper, total + product[None, :, None] * other_sum, total)
        product = jnp.where(upper, product * other_gain, product)
        lower_sum = jnp.where(upper, other_sum, block_sum)
        upper_sum = jnp.where(upper, block_sum, other_sum)
        block_sum = upper_gain[None, :, None] * lower_sum + upper_sum
        block_gain = block_gain * other_gain
        step *= 2
    return total, factors


def butterfly_again(local, factors, axis, reverse):
    count = lax.axis_size(axis)
    me = lax.axis_index(axis)
    place = count - 1 - me if reverse else me
    total = jnp.zeros_like(local)
    block_sum = local
    step = 1
    for product, upper_gain in factors:
        upper = (place // step) % 2 == 1
        got = lax.ppermute(block_sum, axis, [(k, k ^ step) for k in range(count)])
        total = jnp.where(upper, total + product[None, :, None] * got, total)
        lower_sum = jnp.where(upper, got, block_sum)
        upper_sum = jnp.where(upper, block_sum, got)
        block_sum = upper_gain[None, :, None] * lower_sum + upper_sum
        step *= 2
    return total


def batch_sum(value, axis):
    count = lax.axis_size(axis)
    chips = count // 2
    me = lax.axis_index(axis)
    core = me % 2
    chip = me // 2
    shape = value.shape
    flat = value.reshape(-1)
    lanes = 128
    quantum = lanes * 8 * count
    padded_size = -(-flat.shape[0] // quantum) * quantum
    current = jnp.pad(flat, (0, padded_size - flat.shape[0])).reshape(-1, lanes)
    half_rows = current.shape[0] // 2
    partner = [(k, k ^ 1) for k in range(count)]
    keep = lax.dynamic_slice_in_dim(current, core * half_rows, half_rows, 0)
    give = lax.dynamic_slice_in_dim(current, (1 - core) * half_rows, half_rows, 0)
    half = keep + lax.ppermute(give, axis, partner)

    def following(k):
        step = 1 if k % 2 == 0 else -1
        return ((k // 2 + step) % chips) * 2 + k % 2

    ring = [(k, following(k)) for k in range(count)]
    place = jnp.where(core == 0, chip, (chips - chip) % chips)
    pieces = half.reshape(chips, half_rows // chips, lanes)
    for t in range(chips - 1):
        sent = lax.dynamic_index_in_dim(pieces, (place - t) % chips, 0, False)
        got = lax.ppermute(sent, axis, ring)
        slot = (place - t - 1 + chips) % chips
        mine = lax.dynamic_index_in_dim(pieces, slot, 0, False)
        pieces = lax.dynamic_update_index_in_dim(pieces, mine + got, slot, 0)
    for t in range(chips - 1):
        sent = lax.dynamic_index_in_dim(pieces, (place + 1 - t + chips) % chips, 0, False)
        got = lax.ppermute(sent, axis, ring)
        pieces = lax.dynamic_update_index_in_dim(pieces, got, (place - t + chips) % chips, 0)
    half = pieces.reshape(half_rows, lanes)
    other = lax.ppermute(half, axis, partner)
    whole = jnp.zeros_like(current)
    whole = lax.dynamic_update_slice_in_dim(whole, half, core * half_rows, 0)
    whole = lax.dynamic_update_slice_in_dim(whole, other, (1 - core) * half_rows, 0)
    return whole.reshape(-1)[: flat.shape[0]].reshape(shape)


def per_device(initial_state, cotangent, conv_weight, conv_bias, block_gain, adjoint_gain):
    gain_row = block_gain[0]
    back_row = adjoint_gain[0]
    flipped_list = [
        flip_weight(conv_weight[layer_index]) for layer_index in range(conv_weight.shape[0])
    ]
    c_points = initial_state
    following = initial_state
    for sweep_index in range(ITERS):
        ending = relax_block(c_points, conv_weight, conv_bias)[0]
        residual = ending - following
        if sweep_index == 0:
            error, factors = butterfly_first(gain_row, residual, "layer", False)
        else:
            error = butterfly_again(residual, factors, "layer", False)
        c_points = c_points + error
        following = following + gain_row[None, :, None] * error + residual
    ending, stored = relax_block(c_points, conv_weight, conv_bias)
    target = cotangent
    previous = cotangent
    for sweep_index in range(ITERS):
        start_adj = adjoint_block(target, stored, flipped_list)
        residual = start_adj - previous
        if sweep_index == 0:
            error, factors = butterfly_first(back_row, residual, "layer", True)
        else:
            error = butterfly_again(residual, factors, "layer", True)
        target = target + error
        previous = previous + back_row[None, :, None] * error + residual
    adjoint = target
    weight_parts = []
    bias_parts = []
    for layer_index in range(len(stored) - 1, -1, -1):
        adjoint, rounded, scaled = backward_layer(
            adjoint, stored[layer_index][1], flipped_list[layer_index]
        )
        weight_part = jnp.einsum(
            "bop,bkp->ok", rounded, stored[layer_index][0], preferred_element_type=jnp.float32
        )
        bias_part = jnp.sum(scaled, axis=(0, 2))
        weight_parts.insert(0, weight_part)
        bias_parts.insert(0, bias_part)
    width = weight_parts[0].shape[1]
    channels = weight_parts[0].shape[0]
    packed = jnp.stack(
        [
            jnp.concatenate([w, jnp.pad(b, (0, width - channels))[None, :]], axis=0)
            for w, b in zip(weight_parts, bias_parts)
        ]
    )
    packed = batch_sum(packed, "batch")
    weight_grad = packed[:, :channels, :]
    bias_grad = packed[:, channels, :channels]
    return (ending[None], adjoint[None], weight_grad, bias_grad)


def solution(mesh):
    return jax.shard_map(
        per_device,
        mesh=mesh,
        in_specs=(
            P("batch", None, None),
            P("batch", None, None),
            P("layer", None, None),
            P("layer", None),
            P("layer", None),
            P("layer", None),
        ),
        out_specs=(
            P("layer", "batch", None, None),
            P("layer", "batch", None, None),
            P("layer", None, None),
            P("layer", None),
        ),
        check_vma=False,
    )
```

```python
import jax
import jax.numpy as jnp
from jax import lax
from jax.sharding import PartitionSpec as P

HEIGHT = 16
WIDTH = 32
ITERS = 2


step_size = 0.25


def columns(current):
    rounded = current.astype(jnp.bfloat16)
    pixels = HEIGHT * WIDTH
    margin = WIDTH + 1
    padded = jnp.pad(rounded, ((0, 0), (0, 0), (margin, margin)))
    across = jnp.arange(pixels) % WIDTH
    pieces = []
    for offset_y in (-1, 0, 1):
        for offset_x in (-1, 0, 1):
            shift_by = offset_y * WIDTH + offset_x
            inside = (across + offset_x >= 0) & (across + offset_x < WIDTH)
            window = padded[:, :, margin + shift_by : margin + shift_by + pixels]
            pieces.append(jnp.where(inside, window, jnp.zeros_like(window)))
    return jnp.concatenate(pieces, axis=1)


def flip_weight(weight):
    channels = weight.shape[0]
    taps = weight.reshape(channels, 9, channels)[:, ::-1, :]
    return jnp.transpose(taps, (2, 1, 0)).reshape(channels, 9 * channels)


def forward_layer(current, weight, bias_row):
    stacked = columns(current)
    pre_act = (
        jnp.einsum("ok,bkp->bop", weight, stacked, preferred_element_type=jnp.float32)
        + bias_row[None, :, None]
    )
    activity = jnp.tanh(pre_act)
    return (current + step_size * activity, activity, stacked)


def backward_layer(adjoint, activity, flipped):
    scaled = step_size * (1.0 - activity * activity) * adjoint
    rounded = scaled.astype(jnp.bfloat16)
    gathered = columns(rounded)
    back = jnp.einsum("ck,bkp->bcp", flipped, gathered, preferred_element_type=jnp.float32)
    return (adjoint + back, rounded, scaled)


def relax_block(start, weights, biases):
    current = start
    stored = []
    for layer_index in range(weights.shape[0]):
        current, activity, stacked = forward_layer(
            current, weights[layer_index], biases[layer_index]
        )
        stored.append((stacked, activity))
    return (current, stored)


def adjoint_block(finish, stored, flipped_list):
    adjoint = finish
    for layer_index in range(len(stored) - 1, -1, -1):
        adjoint = backward_layer(adjoint, stored[layer_index][1], flipped_list[layer_index])[0]
    return adjoint


def butterfly_first(gain, local, axis, reverse):
    count = lax.axis_size(axis)
    me = lax.axis_index(axis)
    place = count - 1 - me if reverse else me
    channels, pixels = local.shape[1], local.shape[2]
    total = jnp.zeros_like(local)
    product = jnp.ones_like(gain)
    block_sum = local
    block_gain = gain
    factors = []
    step = 1
    while step < count:
        upper = (place // step) % 2 == 1
        gain_row = jnp.pad(block_gain, (0, pixels - channels))
        packed = jnp.concatenate([block_sum, gain_row[None, None, :]], axis=1)
        got = lax.ppermute(packed, axis, [(k, k ^ step) for k in range(count)])
        other_sum = got[:, :channels, :]
        other_gain = got[0, channels, :channels]
        upper_gain = jnp.where(upper, block_gain, other_gain)
        factors.append((product, upper_gain))
        total = jnp.where(upper, total + product[None, :, None] * other_sum, total)
        product = jnp.where(upper, product * other_gain, product)
        lower_sum = jnp.where(upper, other_sum, block_sum)
        upper_sum = jnp.where(upper, block_sum, other_sum)
        block_sum = upper_gain[None, :, None] * lower_sum + upper_sum
        block_gain = block_gain * other_gain
        step *= 2
    return total, factors


def butterfly_again(local, factors, axis, reverse):
    count = lax.axis_size(axis)
    me = lax.axis_index(axis)
    place = count - 1 - me if reverse else me
    total = jnp.zeros_like(local)
    block_sum = local
    step = 1
    for product, upper_gain in factors:
        upper = (place // step) % 2 == 1
        got = lax.ppermute(block_sum, axis, [(k, k ^ step) for k in range(count)])
        total = jnp.where(upper, total + product[None, :, None] * got, total)
        lower_sum = jnp.where(upper, got, block_sum)
        upper_sum = jnp.where(upper, block_sum, got)
        block_sum = upper_gain[None, :, None] * lower_sum + upper_sum
        step *= 2
    return total


def batch_sum(value, axis):
    count = lax.axis_size(axis)
    shape = value.shape
    flat = value.reshape(-1)
    lanes = 128
    quantum = lanes * 8 * count
    padded_size = -(-flat.shape[0] // quantum) * quantum
    slices = jnp.pad(flat, (0, padded_size - flat.shape[0])).reshape(count, -1, lanes)
    mine = jnp.sum(lax.all_to_all(slices, axis, 0, 0), axis=0)
    spread = jnp.broadcast_to(mine[None], slices.shape)
    whole = lax.all_to_all(spread, axis, 0, 0)
    return whole.reshape(-1)[: flat.shape[0]].reshape(shape)


def per_device(initial_state, cotangent, conv_weight, conv_bias, block_gain, adjoint_gain):
    gain_row = block_gain[0]
    back_row = adjoint_gain[0]
    flipped_list = [
        flip_weight(conv_weight[layer_index]) for layer_index in range(conv_weight.shape[0])
    ]
    c_points = initial_state
    following = initial_state
    for sweep_index in range(ITERS):
        ending = relax_block(c_points, conv_weight, conv_bias)[0]
        residual = ending - following
        if sweep_index == 0:
            error, factors = butterfly_first(gain_row, residual, "layer", False)
        else:
            error = butterfly_again(residual, factors, "layer", False)
        c_points = c_points + error
        following = following + gain_row[None, :, None] * error + residual
    ending, stored = relax_block(c_points, conv_weight, conv_bias)
    target = cotangent
    previous = cotangent
    for sweep_index in range(ITERS):
        start_adj = adjoint_block(target, stored, flipped_list)
        residual = start_adj - previous
        if sweep_index == 0:
            error, factors = butterfly_first(back_row, residual, "layer", True)
        else:
            error = butterfly_again(residual, factors, "layer", True)
        target = target + error
        previous = previous + back_row[None, :, None] * error + residual
    adjoint = target
    weight_parts = []
    bias_parts = []
    for layer_index in range(len(stored) - 1, -1, -1):
        adjoint, rounded, scaled = backward_layer(
            adjoint, stored[layer_index][1], flipped_list[layer_index]
        )
        weight_part = jnp.einsum(
            "bop,bkp->ok", rounded, stored[layer_index][0], preferred_element_type=jnp.float32
        )
        bias_part = jnp.sum(scaled, axis=(0, 2))
        weight_parts.insert(0, weight_part)
        bias_parts.insert(0, bias_part)
    width = weight_parts[0].shape[1]
    channels = weight_parts[0].shape[0]
    packed = jnp.stack(
        [
            jnp.concatenate([w, jnp.pad(b, (0, width - channels))[None, :]], axis=0)
            for w, b in zip(weight_parts, bias_parts)
        ]
    )
    packed = batch_sum(packed, "batch")
    weight_grad = packed[:, :channels, :]
    bias_grad = packed[:, channels, :channels]
    return (ending[None], adjoint[None], weight_grad, bias_grad)


def solution(mesh):
    return jax.shard_map(
        per_device,
        mesh=mesh,
        in_specs=(
            P("batch", None, None),
            P("batch", None, None),
            P("layer", None, None),
            P("layer", None),
            P("layer", None),
            P("layer", None),
        ),
        out_specs=(
            P("layer", "batch", None, None),
            P("layer", "batch", None, None),
            P("layer", None, None),
            P("layer", None),
        ),
        check_vma=False,
    )
```

```python
import jax
import jax.numpy as jnp
from jax import lax
from jax.sharding import PartitionSpec as P

HEIGHT = 16
WIDTH = 32
ITERS = 2


step_size = 0.25


def columns(current):
    rounded = current.astype(jnp.bfloat16)
    pixels = HEIGHT * WIDTH
    margin = WIDTH + 1
    padded = jnp.pad(rounded, ((0, 0), (0, 0), (margin, margin)))
    across = jnp.arange(pixels) % WIDTH
    pieces = []
    for offset_y in (-1, 0, 1):
        for offset_x in (-1, 0, 1):
            shift_by = offset_y * WIDTH + offset_x
            inside = (across + offset_x >= 0) & (across + offset_x < WIDTH)
            window = padded[:, :, margin + shift_by : margin + shift_by + pixels]
            pieces.append(jnp.where(inside, window, jnp.zeros_like(window)))
    return jnp.concatenate(pieces, axis=1)


def flip_weight(weight):
    channels = weight.shape[0]
    taps = weight.reshape(channels, 9, channels)[:, ::-1, :]
    return jnp.transpose(taps, (2, 1, 0)).reshape(channels, 9 * channels)


def forward_layer(current, weight, bias_row):
    stacked = columns(current)
    pre_act = (
        jnp.einsum("ok,bkp->bop", weight, stacked, preferred_element_type=jnp.float32)
        + bias_row[None, :, None]
    )
    activity = jnp.tanh(pre_act)
    return (current + step_size * activity, activity, stacked)


def backward_layer(adjoint, activity, flipped):
    scaled = step_size * (1.0 - activity * activity) * adjoint
    rounded = scaled.astype(jnp.bfloat16)
    gathered = columns(rounded)
    back = jnp.einsum("ck,bkp->bcp", flipped, gathered, preferred_element_type=jnp.float32)
    return (adjoint + back, rounded, scaled)


def relax_block(start, weights, biases):
    current = start
    stored = []
    for layer_index in range(weights.shape[0]):
        current, activity, stacked = forward_layer(
            current, weights[layer_index], biases[layer_index]
        )
        stored.append((stacked, activity))
    return (current, stored)


def adjoint_block(finish, stored, flipped_list):
    adjoint = finish
    for layer_index in range(len(stored) - 1, -1, -1):
        adjoint = backward_layer(adjoint, stored[layer_index][1], flipped_list[layer_index])[0]
    return adjoint


def butterfly_first(gain, local, axis, reverse):
    count = lax.axis_size(axis)
    me = lax.axis_index(axis)
    place = count - 1 - me if reverse else me
    channels, pixels = local.shape[1], local.shape[2]
    total = jnp.zeros_like(local)
    product = jnp.ones_like(gain)
    block_sum = local
    block_gain = gain
    factors = []
    step = 1
    while step < count:
        upper = (place // step) % 2 == 1
        gain_row = jnp.pad(block_gain, (0, pixels - channels))
        packed = jnp.concatenate([block_sum, gain_row[None, None, :]], axis=1)
        got = lax.ppermute(packed, axis, [(k, k ^ step) for k in range(count)])
        other_sum = got[:, :channels, :]
        other_gain = got[0, channels, :channels]
        u = upper.astype(gain.dtype)
        upper_gain = jnp.where(upper, block_gain, other_gain)
        taken = u * product
        from_other = upper_gain * u + (1 - u)
        from_own = upper_gain * (1 - u) + u
        factors.append((taken, from_other, from_own))
        total = total + taken[None, :, None] * other_sum
        product = jnp.where(upper, product * other_gain, product)
        block_sum = from_other[None, :, None] * other_sum + from_own[None, :, None] * block_sum
        block_gain = block_gain * other_gain
        step *= 2
    return total, factors


def butterfly_again(local, factors, axis):
    count = lax.axis_size(axis)
    total = jnp.zeros_like(local)
    block_sum = local
    step = 1
    for taken, from_other, from_own in factors:
        got = lax.ppermute(block_sum, axis, [(k, k ^ step) for k in range(count)])
        total = total + taken[None, :, None] * got
        block_sum = from_other[None, :, None] * got + from_own[None, :, None] * block_sum
        step *= 2
    return total


def batch_sum(value, axis):
    count = lax.axis_size(axis)
    chips = count // 2
    me = lax.axis_index(axis)
    core = me % 2
    chip = me // 2
    shape = value.shape
    flat = value.reshape(-1)
    lanes = 128
    quantum = lanes * 8 * count
    padded_size = -(-flat.shape[0] // quantum) * quantum
    current = jnp.pad(flat, (0, padded_size - flat.shape[0])).reshape(-1, lanes)
    half_rows = current.shape[0] // 2
    partner = [(k, k ^ 1) for k in range(count)]
    keep = lax.dynamic_slice_in_dim(current, core * half_rows, half_rows, 0)
    give = lax.dynamic_slice_in_dim(current, (1 - core) * half_rows, half_rows, 0)
    half = keep + lax.ppermute(give, axis, partner)

    def following(k):
        step = 1 if k % 2 == 0 else -1
        return ((k // 2 + step) % chips) * 2 + k % 2

    ring = [(k, following(k)) for k in range(count)]
    place = jnp.where(core == 0, chip, (chips - chip) % chips)
    pieces = half.reshape(chips, half_rows // chips, lanes)
    for t in range(chips - 1):
        sent = lax.dynamic_index_in_dim(pieces, (place - t) % chips, 0, False)
        got = lax.ppermute(sent, axis, ring)
        slot = (place - t - 1 + chips) % chips
        mine = lax.dynamic_index_in_dim(pieces, slot, 0, False)
        pieces = lax.dynamic_update_index_in_dim(pieces, mine + got, slot, 0)
    for t in range(chips - 1):
        sent = lax.dynamic_index_in_dim(pieces, (place + 1 - t + chips) % chips, 0, False)
        got = lax.ppermute(sent, axis, ring)
        pieces = lax.dynamic_update_index_in_dim(pieces, got, (place - t + chips) % chips, 0)
    half = pieces.reshape(half_rows, lanes)
    other = lax.ppermute(half, axis, partner)
    whole = jnp.zeros_like(current)
    whole = lax.dynamic_update_slice_in_dim(whole, half, core * half_rows, 0)
    whole = lax.dynamic_update_slice_in_dim(whole, other, (1 - core) * half_rows, 0)
    return whole.reshape(-1)[: flat.shape[0]].reshape(shape)


def per_device(initial_state, cotangent, conv_weight, conv_bias, block_gain, adjoint_gain):
    gain_row = block_gain[0]
    back_row = adjoint_gain[0]
    flipped_list = [
        flip_weight(conv_weight[layer_index]) for layer_index in range(conv_weight.shape[0])
    ]
    c_points = initial_state
    following = initial_state
    for sweep_index in range(ITERS):
        ending = relax_block(c_points, conv_weight, conv_bias)[0]
        residual = ending - following
        if sweep_index == 0:
            error, factors = butterfly_first(gain_row, residual, "layer", False)
        else:
            error = butterfly_again(residual, factors, "layer")
        c_points = c_points + error
        following = following + gain_row[None, :, None] * error + residual
    ending, stored = relax_block(c_points, conv_weight, conv_bias)
    target = cotangent
    previous = cotangent
    for sweep_index in range(ITERS):
        start_adj = adjoint_block(target, stored, flipped_list)
        residual = start_adj - previous
        if sweep_index == 0:
            error, factors = butterfly_first(back_row, residual, "layer", True)
        else:
            error = butterfly_again(residual, factors, "layer")
        target = target + error
        previous = previous + back_row[None, :, None] * error + residual
    adjoint = target
    weight_parts = []
    bias_parts = []
    for layer_index in range(len(stored) - 1, -1, -1):
        adjoint, rounded, scaled = backward_layer(
            adjoint, stored[layer_index][1], flipped_list[layer_index]
        )
        weight_part = jnp.einsum(
            "bop,bkp->ok", rounded, stored[layer_index][0], preferred_element_type=jnp.float32
        )
        bias_part = jnp.sum(scaled, axis=(0, 2))
        weight_parts.insert(0, weight_part)
        bias_parts.insert(0, bias_part)
    width = weight_parts[0].shape[1]
    channels = weight_parts[0].shape[0]
    packed = jnp.stack(
        [
            jnp.concatenate([w, jnp.pad(b, (0, width - channels))[None, :]], axis=0)
            for w, b in zip(weight_parts, bias_parts)
        ]
    )
    packed = batch_sum(packed, "batch")
    weight_grad = packed[:, :channels, :]
    bias_grad = packed[:, channels, :channels]
    return (ending[None], adjoint[None], weight_grad, bias_grad)


def solution(mesh):
    return jax.shard_map(
        per_device,
        mesh=mesh,
        in_specs=(
            P("batch", None, None),
            P("batch", None, None),
            P("layer", None, None),
            P("layer", None),
            P("layer", None),
            P("layer", None),
        ),
        out_specs=(
            P("layer", "batch", None, None),
            P("layer", "batch", None, None),
            P("layer", None, None),
            P("layer", None),
        ),
        check_vma=False,
    )
```

```python
import jax
import jax.numpy as jnp
from jax import lax
from jax.sharding import PartitionSpec as P

HEIGHT = 16
WIDTH = 32
ITERS = 2


step_size = 0.25


def columns(current):
    rounded = current.astype(jnp.bfloat16)
    pixels = HEIGHT * WIDTH
    margin = WIDTH + 1
    padded = jnp.pad(rounded, ((0, 0), (0, 0), (margin, margin)))
    across = jnp.arange(pixels) % WIDTH
    pieces = []
    for offset_y in (-1, 0, 1):
        for offset_x in (-1, 0, 1):
            shift_by = offset_y * WIDTH + offset_x
            inside = (across + offset_x >= 0) & (across + offset_x < WIDTH)
            window = padded[:, :, margin + shift_by : margin + shift_by + pixels]
            pieces.append(jnp.where(inside, window, jnp.zeros_like(window)))
    return jnp.concatenate(pieces, axis=1)


def flip_weight(weight):
    channels = weight.shape[0]
    taps = weight.reshape(channels, 9, channels)[:, ::-1, :]
    return jnp.transpose(taps, (2, 1, 0)).reshape(channels, 9 * channels)


def forward_layer(current, weight, bias_row):
    stacked = columns(current)
    pre_act = (
        jnp.einsum("ok,bkp->bop", weight, stacked, preferred_element_type=jnp.float32)
        + bias_row[None, :, None]
    )
    activity = jnp.tanh(pre_act)
    return (current + step_size * activity, activity, stacked)


def backward_layer(adjoint, activity, flipped):
    scaled = step_size * (1.0 - activity * activity) * adjoint
    rounded = scaled.astype(jnp.bfloat16)
    gathered = columns(rounded)
    back = jnp.einsum("ck,bkp->bcp", flipped, gathered, preferred_element_type=jnp.float32)
    return (adjoint + back, rounded, scaled)


def relax_block(start, weights, biases):
    current = start
    stored = []
    for layer_index in range(weights.shape[0]):
        current, activity, stacked = forward_layer(
            current, weights[layer_index], biases[layer_index]
        )
        stored.append((stacked, activity))
    return (current, stored)


def adjoint_block(finish, stored, flipped_list):
    adjoint = finish
    for layer_index in range(len(stored) - 1, -1, -1):
        adjoint = backward_layer(adjoint, stored[layer_index][1], flipped_list[layer_index])[0]
    return adjoint


def gain_factors(place, step, block_gain, other_gain, product, upper_dtype):
    upper = (place // step) % 2 == 1
    u = upper.astype(upper_dtype)
    upper_gain = jnp.where(upper, block_gain, other_gain)
    taken = u * product
    from_other = upper_gain * u + (1 - u)
    from_own = upper_gain * (1 - u) + u
    product = jnp.where(upper, product * other_gain, product)
    return (taken, from_other, from_own), product, block_gain * other_gain


def butterfly_first(gain, local, axis, other_gain_row):
    count = lax.axis_size(axis)
    me = lax.axis_index(axis)
    channels, pixels = local.shape[1], local.shape[2]
    total = jnp.zeros_like(local)
    block_sum = local
    states = [
        [me, gain, jnp.ones_like(gain), []],
        [count - 1 - me, other_gain_row, jnp.ones_like(other_gain_row), []],
    ]
    step = 1
    while step < count:
        rows = [jnp.pad(state[1], (0, pixels - channels))[None, None, :] for state in states]
        packed = jnp.concatenate([block_sum] + rows, axis=1)
        got = lax.ppermute(packed, axis, [(k, k ^ step) for k in range(count)])
        other_sum = got[:, :channels, :]
        for i, state in enumerate(states):
            factor, state[2], new_gain = gain_factors(
                state[0], step, state[1], got[0, channels + i, :channels], state[2], gain.dtype
            )
            state[1] = new_gain
            state[3].append(factor)
        taken, from_other, from_own = states[0][3][-1]
        total = total + taken[None, :, None] * other_sum
        block_sum = from_other[None, :, None] * other_sum + from_own[None, :, None] * block_sum
        step *= 2
    return total, states[0][3], states[1][3]


def butterfly_again(local, factors, axis):
    count = lax.axis_size(axis)
    total = jnp.zeros_like(local)
    block_sum = local
    step = 1
    for taken, from_other, from_own in factors:
        got = lax.ppermute(block_sum, axis, [(k, k ^ step) for k in range(count)])
        total = total + taken[None, :, None] * got
        block_sum = from_other[None, :, None] * got + from_own[None, :, None] * block_sum
        step *= 2
    return total


def batch_sum(value, axis):
    count = lax.axis_size(axis)
    chips = count // 2
    me = lax.axis_index(axis)
    core = me % 2
    chip = me // 2
    shape = value.shape
    flat = value.reshape(-1)
    lanes = 128
    quantum = lanes * 8 * count
    padded_size = -(-flat.shape[0] // quantum) * quantum
    current = jnp.pad(flat, (0, padded_size - flat.shape[0])).reshape(-1, lanes)
    half_rows = current.shape[0] // 2
    partner = [(k, k ^ 1) for k in range(count)]
    keep = lax.dynamic_slice_in_dim(current, core * half_rows, half_rows, 0)
    give = lax.dynamic_slice_in_dim(current, (1 - core) * half_rows, half_rows, 0)
    half = keep + lax.ppermute(give, axis, partner)

    def following(k):
        step = 1 if k % 2 == 0 else -1
        return ((k // 2 + step) % chips) * 2 + k % 2

    ring = [(k, following(k)) for k in range(count)]
    place = jnp.where(core == 0, chip, (chips - chip) % chips)
    pieces = half.reshape(chips, half_rows // chips, lanes)
    for t in range(chips - 1):
        sent = lax.dynamic_index_in_dim(pieces, (place - t) % chips, 0, False)
        got = lax.ppermute(sent, axis, ring)
        slot = (place - t - 1 + chips) % chips
        mine = lax.dynamic_index_in_dim(pieces, slot, 0, False)
        pieces = lax.dynamic_update_index_in_dim(pieces, mine + got, slot, 0)
    for t in range(chips - 1):
        sent = lax.dynamic_index_in_dim(pieces, (place + 1 - t + chips) % chips, 0, False)
        got = lax.ppermute(sent, axis, ring)
        pieces = lax.dynamic_update_index_in_dim(pieces, got, (place - t + chips) % chips, 0)
    half = pieces.reshape(half_rows, lanes)
    other = lax.ppermute(half, axis, partner)
    whole = jnp.zeros_like(current)
    whole = lax.dynamic_update_slice_in_dim(whole, half, core * half_rows, 0)
    whole = lax.dynamic_update_slice_in_dim(whole, other, (1 - core) * half_rows, 0)
    return whole.reshape(-1)[: flat.shape[0]].reshape(shape)


def per_device(initial_state, cotangent, conv_weight, conv_bias, block_gain, adjoint_gain):
    gain_row = block_gain[0]
    back_row = adjoint_gain[0]
    flipped_list = [
        flip_weight(conv_weight[layer_index]) for layer_index in range(conv_weight.shape[0])
    ]
    c_points = initial_state
    following = initial_state
    for sweep_index in range(ITERS):
        ending = relax_block(c_points, conv_weight, conv_bias)[0]
        residual = ending - following
        if sweep_index == 0:
            error, factors, back_factors = butterfly_first(gain_row, residual, "layer", back_row)
        else:
            error = butterfly_again(residual, factors, "layer")
        c_points = c_points + error
        following = following + gain_row[None, :, None] * error + residual
    ending, stored = relax_block(c_points, conv_weight, conv_bias)
    target = cotangent
    previous = cotangent
    for sweep_index in range(ITERS):
        start_adj = adjoint_block(target, stored, flipped_list)
        residual = start_adj - previous
        error = butterfly_again(residual, back_factors, "layer")
        target = target + error
        previous = previous + back_row[None, :, None] * error + residual
    adjoint = target
    weight_parts = []
    bias_parts = []
    for layer_index in range(len(stored) - 1, -1, -1):
        adjoint, rounded, scaled = backward_layer(
            adjoint, stored[layer_index][1], flipped_list[layer_index]
        )
        weight_part = jnp.einsum(
            "bop,bkp->ok", rounded, stored[layer_index][0], preferred_element_type=jnp.float32
        )
        bias_part = jnp.sum(scaled, axis=(0, 2))
        weight_parts.insert(0, weight_part)
        bias_parts.insert(0, bias_part)
    width = weight_parts[0].shape[1]
    channels = weight_parts[0].shape[0]
    packed = jnp.stack(
        [
            jnp.concatenate([w, jnp.pad(b, (0, width - channels))[None, :]], axis=0)
            for w, b in zip(weight_parts, bias_parts)
        ]
    )
    packed = batch_sum(packed, "batch")
    weight_grad = packed[:, :channels, :]
    bias_grad = packed[:, channels, :channels]
    return (ending[None], adjoint[None], weight_grad, bias_grad)


def solution(mesh):
    return jax.shard_map(
        per_device,
        mesh=mesh,
        in_specs=(
            P("batch", None, None),
            P("batch", None, None),
            P("layer", None, None),
            P("layer", None),
            P("layer", None),
            P("layer", None),
        ),
        out_specs=(
            P("layer", "batch", None, None),
            P("layer", "batch", None, None),
            P("layer", None, None),
            P("layer", None),
        ),
        check_vma=False,
    )
```

```python
import jax
import jax.numpy as jnp
from jax import lax
from jax.sharding import PartitionSpec as P

HEIGHT = 16
WIDTH = 32
ITERS = 2


step_size = 0.25


def columns(current):
    rounded = current.astype(jnp.bfloat16)
    pixels = HEIGHT * WIDTH
    margin = WIDTH + 1
    padded = jnp.pad(rounded, ((0, 0), (0, 0), (margin, margin)))
    across = jnp.arange(pixels) % WIDTH
    pieces = []
    for offset_y in (-1, 0, 1):
        for offset_x in (-1, 0, 1):
            shift_by = offset_y * WIDTH + offset_x
            inside = (across + offset_x >= 0) & (across + offset_x < WIDTH)
            window = padded[:, :, margin + shift_by : margin + shift_by + pixels]
            pieces.append(jnp.where(inside, window, jnp.zeros_like(window)))
    return jnp.concatenate(pieces, axis=1)


def flip_weight(weight):
    channels = weight.shape[0]
    taps = weight.reshape(channels, 9, channels)[:, ::-1, :]
    return jnp.transpose(taps, (2, 1, 0)).reshape(channels, 9 * channels)


def forward_layer(current, weight, bias_row):
    stacked = columns(current)
    pre_act = (
        jnp.einsum("ok,bkp->bop", weight, stacked, preferred_element_type=jnp.float32)
        + bias_row[None, :, None]
    )
    activity = jnp.tanh(pre_act)
    return (current + step_size * activity, activity, stacked)


def backward_layer(adjoint, activity, flipped):
    scaled = step_size * (1.0 - activity * activity) * adjoint
    rounded = scaled.astype(jnp.bfloat16)
    gathered = columns(rounded)
    back = jnp.einsum("ck,bkp->bcp", flipped, gathered, preferred_element_type=jnp.float32)
    return (adjoint + back, rounded, scaled)


def relax_block(start, weights, biases):
    current = start
    stored = []
    for layer_index in range(weights.shape[0]):
        current, activity, stacked = forward_layer(
            current, weights[layer_index], biases[layer_index]
        )
        stored.append((stacked, activity))
    return (current, stored)


def adjoint_block(finish, stored, flipped_list):
    adjoint = finish
    for layer_index in range(len(stored) - 1, -1, -1):
        adjoint = backward_layer(adjoint, stored[layer_index][1], flipped_list[layer_index])[0]
    return adjoint


def gain_factors(place, step, block_gain, other_gain, product, upper_dtype):
    upper = (place // step) % 2 == 1
    u = upper.astype(upper_dtype)
    upper_gain = jnp.where(upper, block_gain, other_gain)
    taken = u * product
    from_other = upper_gain * u + (1 - u)
    from_own = upper_gain * (1 - u) + u
    product = jnp.where(upper, product * other_gain, product)
    return (taken, from_other, from_own), product, block_gain * other_gain


def gain_butterfly(gains, axis):
    count = lax.axis_size(axis)
    me = lax.axis_index(axis)
    places = [me, count - 1 - me]
    block = gains
    products = [jnp.ones_like(gains[0]), jnp.ones_like(gains[1])]
    factors = [[], []]
    step = 1
    while step < count:
        got = lax.ppermute(block, axis, [(k, k ^ step) for k in range(count)])
        rows = []
        for i in range(2):
            factor, products[i], new_gain = gain_factors(
                places[i], step, block[i], got[i], products[i], gains.dtype
            )
            factors[i].append(factor)
            rows.append(new_gain)
        block = jnp.stack(rows)
        step *= 2
    return factors[0], factors[1]


def butterfly_again(local, factors, axis):
    count = lax.axis_size(axis)
    total = jnp.zeros_like(local)
    block_sum = local
    step = 1
    for taken, from_other, from_own in factors:
        got = lax.ppermute(block_sum, axis, [(k, k ^ step) for k in range(count)])
        total = total + taken[None, :, None] * got
        block_sum = from_other[None, :, None] * got + from_own[None, :, None] * block_sum
        step *= 2
    return total


def batch_sum(value, axis):
    count = lax.axis_size(axis)
    chips = count // 2
    me = lax.axis_index(axis)
    core = me % 2
    chip = me // 2
    shape = value.shape
    flat = value.reshape(-1)
    lanes = 128
    quantum = lanes * 8 * count
    padded_size = -(-flat.shape[0] // quantum) * quantum
    current = jnp.pad(flat, (0, padded_size - flat.shape[0])).reshape(-1, lanes)
    half_rows = current.shape[0] // 2
    partner = [(k, k ^ 1) for k in range(count)]
    keep = lax.dynamic_slice_in_dim(current, core * half_rows, half_rows, 0)
    give = lax.dynamic_slice_in_dim(current, (1 - core) * half_rows, half_rows, 0)
    half = keep + lax.ppermute(give, axis, partner)

    def following(k):
        step = 1 if k % 2 == 0 else -1
        return ((k // 2 + step) % chips) * 2 + k % 2

    ring = [(k, following(k)) for k in range(count)]
    place = jnp.where(core == 0, chip, (chips - chip) % chips)
    pieces = half.reshape(chips, half_rows // chips, lanes)
    for t in range(chips - 1):
        sent = lax.dynamic_index_in_dim(pieces, (place - t) % chips, 0, False)
        got = lax.ppermute(sent, axis, ring)
        slot = (place - t - 1 + chips) % chips
        mine = lax.dynamic_index_in_dim(pieces, slot, 0, False)
        pieces = lax.dynamic_update_index_in_dim(pieces, mine + got, slot, 0)
    for t in range(chips - 1):
        sent = lax.dynamic_index_in_dim(pieces, (place + 1 - t + chips) % chips, 0, False)
        got = lax.ppermute(sent, axis, ring)
        pieces = lax.dynamic_update_index_in_dim(pieces, got, (place - t + chips) % chips, 0)
    half = pieces.reshape(half_rows, lanes)
    other = lax.ppermute(half, axis, partner)
    whole = jnp.zeros_like(current)
    whole = lax.dynamic_update_slice_in_dim(whole, half, core * half_rows, 0)
    whole = lax.dynamic_update_slice_in_dim(whole, other, (1 - core) * half_rows, 0)
    return whole.reshape(-1)[: flat.shape[0]].reshape(shape)


def per_device(initial_state, cotangent, conv_weight, conv_bias, block_gain, adjoint_gain):
    gain_row = block_gain[0]
    back_row = adjoint_gain[0]
    flipped_list = [
        flip_weight(conv_weight[layer_index]) for layer_index in range(conv_weight.shape[0])
    ]
    factors, back_factors = gain_butterfly(jnp.stack([gain_row, back_row]), "layer")
    c_points = initial_state
    following = initial_state
    for sweep_index in range(ITERS):
        ending = relax_block(c_points, conv_weight, conv_bias)[0]
        residual = ending - following
        error = butterfly_again(residual, factors, "layer")
        c_points = c_points + error
        following = following + gain_row[None, :, None] * error + residual
    ending, stored = relax_block(c_points, conv_weight, conv_bias)
    target = cotangent
    previous = cotangent
    for sweep_index in range(ITERS):
        start_adj = adjoint_block(target, stored, flipped_list)
        residual = start_adj - previous
        error = butterfly_again(residual, back_factors, "layer")
        target = target + error
        previous = previous + back_row[None, :, None] * error + residual
    adjoint = target
    weight_parts = []
    bias_parts = []
    for layer_index in range(len(stored) - 1, -1, -1):
        adjoint, rounded, scaled = backward_layer(
            adjoint, stored[layer_index][1], flipped_list[layer_index]
        )
        weight_part = jnp.einsum(
            "bop,bkp->ok", rounded, stored[layer_index][0], preferred_element_type=jnp.float32
        )
        bias_part = jnp.sum(scaled, axis=(0, 2))
        weight_parts.insert(0, weight_part)
        bias_parts.insert(0, bias_part)
    width = weight_parts[0].shape[1]
    channels = weight_parts[0].shape[0]
    packed = jnp.stack(
        [
            jnp.concatenate([w, jnp.pad(b, (0, width - channels))[None, :]], axis=0)
            for w, b in zip(weight_parts, bias_parts)
        ]
    )
    packed = batch_sum(packed, "batch")
    weight_grad = packed[:, :channels, :]
    bias_grad = packed[:, channels, :channels]
    return (ending[None], adjoint[None], weight_grad, bias_grad)


def solution(mesh):
    return jax.shard_map(
        per_device,
        mesh=mesh,
        in_specs=(
            P("batch", None, None),
            P("batch", None, None),
            P("layer", None, None),
            P("layer", None),
            P("layer", None),
            P("layer", None),
        ),
        out_specs=(
            P("layer", "batch", None, None),
            P("layer", "batch", None, None),
            P("layer", None, None),
            P("layer", None),
        ),
        check_vma=False,
    )
```

```python
import jax
import jax.numpy as jnp
from jax import lax
from jax.sharding import PartitionSpec as P

HEIGHT = 16
WIDTH = 32
ITERS = 2


step_size = 0.25


def columns(current):
    rounded = current.astype(jnp.bfloat16)
    pixels = HEIGHT * WIDTH
    margin = WIDTH + 1
    padded = jnp.pad(rounded, ((0, 0), (0, 0), (margin, margin)))
    across = jnp.arange(pixels) % WIDTH
    pieces = []
    for offset_y in (-1, 0, 1):
        for offset_x in (-1, 0, 1):
            shift_by = offset_y * WIDTH + offset_x
            inside = (across + offset_x >= 0) & (across + offset_x < WIDTH)
            window = padded[:, :, margin + shift_by : margin + shift_by + pixels]
            pieces.append(jnp.where(inside, window, jnp.zeros_like(window)))
    return jnp.concatenate(pieces, axis=1)


def flip_weight(weight):
    channels = weight.shape[0]
    taps = weight.reshape(channels, 9, channels)[:, ::-1, :]
    return jnp.transpose(taps, (2, 1, 0)).reshape(channels, 9 * channels)


def forward_layer(current, weight, bias_row):
    stacked = columns(current)
    pre_act = (
        jnp.einsum("ok,bkp->bop", weight, stacked, preferred_element_type=jnp.float32)
        + bias_row[None, :, None]
    )
    activity = jnp.tanh(pre_act)
    return (current + step_size * activity, activity, stacked)


def backward_layer(adjoint, activity, flipped):
    scaled = step_size * (1.0 - activity * activity) * adjoint
    rounded = scaled.astype(jnp.bfloat16)
    gathered = columns(rounded)
    back = jnp.einsum("ck,bkp->bcp", flipped, gathered, preferred_element_type=jnp.float32)
    return (adjoint + back, rounded, scaled)


def relax_block(start, weights, biases):
    current = start
    stored = []
    for layer_index in range(weights.shape[0]):
        current, activity, stacked = forward_layer(
            current, weights[layer_index], biases[layer_index]
        )
        stored.append((stacked, activity))
    return (current, stored)


def adjoint_block(finish, stored, flipped_list):
    adjoint = finish
    for layer_index in range(len(stored) - 1, -1, -1):
        adjoint = backward_layer(adjoint, stored[layer_index][1], flipped_list[layer_index])[0]
    return adjoint


def gain_factors(place, step, block_gain, other_gain, product, upper_dtype):
    upper = (place // step) % 2 == 1
    u = upper.astype(upper_dtype)
    upper_gain = jnp.where(upper, block_gain, other_gain)
    taken = u * product
    from_other = upper_gain * u + (1 - u)
    from_own = upper_gain * (1 - u) + u
    product = jnp.where(upper, product * other_gain, product)
    return (taken, from_other, from_own), product, block_gain * other_gain


def butterfly_first(gain, local, axis, other_gain_row):
    count = lax.axis_size(axis)
    me = lax.axis_index(axis)
    channels, pixels = local.shape[1], local.shape[2]
    total = jnp.zeros_like(local)
    block_sum = local
    states = [
        [me, gain, jnp.ones_like(gain), []],
        [count - 1 - me, other_gain_row, jnp.ones_like(other_gain_row), []],
    ]
    step = 1
    while step < count:
        rows = [jnp.pad(state[1], (0, pixels - channels))[None, None, :] for state in states]
        packed = jnp.concatenate([block_sum] + rows, axis=1)
        got = lax.ppermute(packed, axis, [(k, k ^ step) for k in range(count)])
        other_sum = got[:, :channels, :]
        for i, state in enumerate(states):
            factor, state[2], new_gain = gain_factors(
                state[0], step, state[1], got[0, channels + i, :channels], state[2], gain.dtype
            )
            state[1] = new_gain
            state[3].append(factor)
        taken, from_other, from_own = states[0][3][-1]
        total = total + taken[None, :, None] * other_sum
        block_sum = from_other[None, :, None] * other_sum + from_own[None, :, None] * block_sum
        step *= 2
    return total, states[0][3], states[1][3]


def butterfly_again(local, factors, axis):
    count = lax.axis_size(axis)
    total = jnp.zeros_like(local)
    block_sum = local
    step = 1
    for taken, from_other, from_own in factors:
        got = lax.ppermute(block_sum, axis, [(k, k ^ step) for k in range(count)])
        total = total + taken[None, :, None] * got
        block_sum = from_other[None, :, None] * got + from_own[None, :, None] * block_sum
        step *= 2
    return total


def batch_sum(value, axis):
    count = lax.axis_size(axis)
    chips = count // 2
    me = lax.axis_index(axis)
    core = me % 2
    chip = me // 2
    shape = value.shape
    flat = value.reshape(-1)
    lanes = 128
    quantum = lanes * 8 * count
    padded_size = -(-flat.shape[0] // quantum) * quantum
    current = jnp.pad(flat, (0, padded_size - flat.shape[0])).reshape(-1, lanes)
    half_rows = current.shape[0] // 2
    partner = [(k, k ^ 1) for k in range(count)]
    keep = lax.dynamic_slice_in_dim(current, core * half_rows, half_rows, 0)
    give = lax.dynamic_slice_in_dim(current, (1 - core) * half_rows, half_rows, 0)
    half = keep + lax.ppermute(give, axis, partner)

    def following(k):
        step = 1 if k % 2 == 0 else -1
        return ((k // 2 + step) % chips) * 2 + k % 2

    ring = [(k, following(k)) for k in range(count)]
    place = jnp.where(core == 0, chip, (chips - chip) % chips)
    pieces = half.reshape(chips, half_rows // chips, lanes)
    doubled = jnp.concatenate([pieces, pieces], axis=0)
    pieces = lax.dynamic_slice_in_dim(doubled, place, chips, 0)
    slots = list(pieces)
    for t in range(chips - 1):
        got = lax.ppermute(slots[(-t) % chips], axis, ring)
        slot = (-t - 1) % chips
        slots[slot] = slots[slot] + got
    for t in range(chips - 1):
        slots[(-t) % chips] = lax.ppermute(slots[(1 - t) % chips], axis, ring)
    rotated = jnp.stack(slots)
    doubled = jnp.concatenate([rotated, rotated], axis=0)
    pieces = lax.dynamic_slice_in_dim(doubled, (chips - place) % chips, chips, 0)
    half = pieces.reshape(half_rows, lanes)
    other = lax.ppermute(half, axis, partner)
    whole = jnp.zeros_like(current)
    whole = lax.dynamic_update_slice_in_dim(whole, half, core * half_rows, 0)
    whole = lax.dynamic_update_slice_in_dim(whole, other, (1 - core) * half_rows, 0)
    return whole.reshape(-1)[: flat.shape[0]].reshape(shape)


def per_device(initial_state, cotangent, conv_weight, conv_bias, block_gain, adjoint_gain):
    gain_row = block_gain[0]
    back_row = adjoint_gain[0]
    flipped_list = [
        flip_weight(conv_weight[layer_index]) for layer_index in range(conv_weight.shape[0])
    ]
    c_points = initial_state
    following = initial_state
    for sweep_index in range(ITERS):
        ending = relax_block(c_points, conv_weight, conv_bias)[0]
        residual = ending - following
        if sweep_index == 0:
            error, factors, back_factors = butterfly_first(gain_row, residual, "layer", back_row)
        else:
            error = butterfly_again(residual, factors, "layer")
        c_points = c_points + error
        following = following + gain_row[None, :, None] * error + residual
    ending, stored = relax_block(c_points, conv_weight, conv_bias)
    target = cotangent
    previous = cotangent
    for sweep_index in range(ITERS):
        start_adj = adjoint_block(target, stored, flipped_list)
        residual = start_adj - previous
        error = butterfly_again(residual, back_factors, "layer")
        target = target + error
        previous = previous + back_row[None, :, None] * error + residual
    adjoint = target
    weight_parts = []
    bias_parts = []
    for layer_index in range(len(stored) - 1, -1, -1):
        adjoint, rounded, scaled = backward_layer(
            adjoint, stored[layer_index][1], flipped_list[layer_index]
        )
        weight_part = jnp.einsum(
            "bop,bkp->ok", rounded, stored[layer_index][0], preferred_element_type=jnp.float32
        )
        bias_part = jnp.sum(scaled, axis=(0, 2))
        weight_parts.insert(0, weight_part)
        bias_parts.insert(0, bias_part)
    width = weight_parts[0].shape[1]
    channels = weight_parts[0].shape[0]
    packed = jnp.stack(
        [
            jnp.concatenate([w, jnp.pad(b, (0, width - channels))[None, :]], axis=0)
            for w, b in zip(weight_parts, bias_parts)
        ]
    )
    packed = batch_sum(packed, "batch")
    weight_grad = packed[:, :channels, :]
    bias_grad = packed[:, channels, :channels]
    return (ending[None], adjoint[None], weight_grad, bias_grad)


def solution(mesh):
    return jax.shard_map(
        per_device,
        mesh=mesh,
        in_specs=(
            P("batch", None, None),
            P("batch", None, None),
            P("layer", None, None),
            P("layer", None),
            P("layer", None),
            P("layer", None),
        ),
        out_specs=(
            P("layer", "batch", None, None),
            P("layer", "batch", None, None),
            P("layer", None, None),
            P("layer", None),
        ),
        check_vma=False,
    )
```
